32 devices in a mesh: parts: 2 (over y), filt: 4 (over z), space: 4 (over x, core).
Axes of the slice: x: 2, y: 2, z: 4, core: 2. Of those that a mesh axis runs over, the one named last changes fastest.
Arguments:
- volume: bfloat16 [512, 16, 8, 128], P('filt', ('parts', 'space')), parts along dimension 1, may hold values from -6 to 6
- weight: bfloat16 [512, 27, 512], P('filt'), may hold values from -0.0546875 to 0.0546875
- bias: float32 [512], P('filt'), may hold values from -3 to 3
- upstream: bfloat16 [512, 16, 8, 128], P('filt', ('parts', 'space')), parts along dimension 1, may hold values from -0.0625 to 0.0625
Outputs:
- features: bfloat16 [512, 16, 8, 128], P('filt', ('parts', 'space')), parts along dimension 1
- weight_grad: float32 [1024, 27, 512], P(('parts', 'filt')), parts along dimension 0
The draws below stay inside these ranges and needn't reach their ends.
There are 2 independent parts, one for each index of `parts`. The reference program is written for one: setup_inputs(seed, part) draws one part's arguments, and reference() takes and returns one part's arrays. A program takes and returns all parts, laid end to end along the dimension named above; an argument that names none is the same for every part. Nothing has to cross between parts.
All inputs are finite; a program needn't handle non-finite values.
Results may differ from the reference program's by a relative error of at most 0.001.
Values may be sent and summed in bfloat16 or wider, within the bound.
No kernel may reach another device: no remote copies, remote signals or barrier semaphores. Data moves between devices by JAX's collectives and lax.ppermute only.
A program may use at most 128 MiB of HBM per device.

```python
import jax
import jax.numpy as jnp
from jax import lax

CIN = 512
COUT = 512
TAPS = 27
NY = 8
NZ = 128
NX = 8


def block_scale(rng, extent, shards, smallest, top_value):
    factor_of, own = 1.0, jax.random.fold_in(rng, 6)
    for axis_at, shards_of in shards:
        steps = jnp.exp(jax.random.uniform(jax.random.fold_in(own, axis_at), (shards_of,), jnp.float32, smallest / len(shards), top_value / len(shards)))
        factor_of = factor_of * jnp.repeat(steps, extent[axis_at] // shards_of).reshape([-1 if axis == axis_at else 1 for axis in range(len(extent))])
    return factor_of


def centred(own_key, shape, scale, most, shards=(), dtype=jnp.bfloat16):
    gain = block_scale(own_key, shape, shards, -0.22, 0.18) if shards else 1.0
    drawn = jax.random.normal(own_key, shape, jnp.float32) * scale * gain
    return jnp.minimum(jnp.maximum(drawn, -most), most).astype(dtype)


def setup_inputs(seed: int = 0, part: int = 0) -> dict:
    splits = jax.random.split(jax.random.key(seed), 5)
    part_splits = jax.random.split(jax.random.fold_in(splits[4], part), 5)
    return {
        "volume": centred(part_splits[0], (CIN, NX, NY, NZ), 1.0, 6.0, ((0, 4), (1, 4))),
        "weight": centred(splits[1], (COUT, TAPS, CIN), (TAPS * CIN) ** -0.5, 0.0546875, ((0, 4),)),
        "bias": centred(splits[2], (COUT,), 0.5, 3.0, ((0, 4),), jnp.float32),
        "upstream": centred(part_splits[3], (COUT, NX, NY, NZ), (NX * NY * NZ) ** -0.5, 0.0625, ((0, 4), (1, 4))),
    }


def reference(volume, weight, bias, upstream):
    kernel = weight.reshape(COUT, 3, 3, 3, CIN).transpose(0, 4, 1, 2, 3)
    pre = lax.conv_general_dilated(volume[None], kernel, (1, 1, 1), [(1, 1), (1, 1), (1, 1)], dimension_numbers=("NCDHW", "OIDHW", "NCDHW"), preferred_element_type=jnp.float32)[0]
    pre = pre + bias[:, None, None, None]
    features = jnp.where(pre > 0, pre, 0.3 * pre).astype(jnp.bfloat16)
    padded = jnp.pad(volume, ((0, 0), (1, 1), (1, 1), (1, 1))).astype(jnp.float32)
    slope = upstream.astype(jnp.float32)
    columns = []
    for tap in range(27):
        first = tap // 9
        second = (tap // 3) % 3
        third = tap % 3
        window = padded[:, first:first + NX, second:second + NY, third:third + NZ]
        columns.append(jnp.einsum("oxyz,cxyz->oc", slope, window))
    weight_grad = jnp.stack(columns, 1)
    return features, weight_grad
```

```python
import jax
import jax.numpy as jnp
from jax import lax
from jax.sharding import PartitionSpec as P


def padded(block, sides, width):
    for axis, dim in sides:
        count = lax.axis_size(axis)
        forward = [(i, i + 1) for i in range(count - 1)]
        backward = [(target, source) for source, target in forward]
        low = lax.ppermute(
            lax.slice_in_dim(block, block.shape[dim] - width, None, axis=dim), axis, forward
        )
        high = lax.ppermute(lax.slice_in_dim(block, 0, width, axis=dim), axis, backward)
        block = jnp.concatenate([low, block, high], axis=dim)
    return block


def convolve(slab, kernel):
    return lax.conv_general_dilated(
        slab[None],
        kernel,
        (1, 1, 1),
        [(0, 0), (1, 1), (1, 1)],
        dimension_numbers=("NCDHW", "OIDHW", "NCDHW"),
        preferred_element_type=jnp.float32,
    )[0]


def plane_shifts(upstream):
    height = upstream.shape[2]
    length = upstream.shape[3]
    spread = jnp.pad(upstream, ((0, 0), (0, 0), (1, 1), (1, 1)))
    copies = []
    for tap in range(9):
        second = tap // 3
        third = tap % 3
        copies.append(
            spread[:, :, 2 - second : 2 - second + height, 2 - third : 2 - third + length]
        )
    stacked = jnp.stack(copies, 1)
    return stacked.reshape(upstream.shape[0] * 9, -1)


def tap_grads(rimmed, upstream):
    out_dev = upstream.shape[0]
    depth = upstream.shape[1]
    shifted = plane_shifts(upstream)
    rows = []
    for first in range(3):
        window = lax.slice_in_dim(rimmed, first, first + depth, axis=1)
        flat = window.reshape(window.shape[0], -1)
        product = lax.dot_general(
            shifted, flat, (((1,), (1,)), ((), ())), preferred_element_type=jnp.float32
        )
        rows.append(product.reshape(out_dev, 9, window.shape[0]))
    return jnp.concatenate(rows, axis=1)


def space_sum(grads):
    count = lax.axis_size("space")
    if count != 4 or grads.shape[2] % 2:
        return lax.psum(grads, "space")
    here = lax.axis_index("space")
    core = here % 2
    half = grads.shape[2] // 2
    pair = [(i, i ^ 1) for i in range(count)]
    across = [(i, i ^ 2) for i in range(count)]
    mine = lax.dynamic_slice_in_dim(grads, core * half, half, axis=2)
    other = lax.dynamic_slice_in_dim(grads, (1 - core) * half, half, axis=2)
    mine = mine + lax.ppermute(other, "space", pair)
    mine = mine + lax.ppermute(mine, "space", across)
    theirs = lax.ppermute(mine, "space", pair)
    low = jnp.where(core == 0, mine, theirs)
    high = jnp.where(core == 0, theirs, mine)
    return jnp.concatenate([low, high], axis=2)


def on_device(volume, weight, bias, upstream):
    out_dev = weight.shape[0]
    in_all = weight.shape[2]
    kernel = weight.reshape(out_dev, 3, 3, 3, in_all).transpose(0, 4, 1, 2, 3)
    whole = lax.all_gather(volume, "filt", axis=0, tiled=True)
    rimmed = padded(whole, (("space", 1),), 1)
    weight_grad = space_sum(tap_grads(rimmed, upstream))
    pre = convolve(rimmed, kernel)
    pre = pre + bias[:, None, None, None]
    features = jnp.where(pre > 0, pre, 0.3 * pre).astype(jnp.bfloat16)
    return (features, weight_grad)


def solution(mesh):
    return jax.shard_map(
        on_device,
        mesh=mesh,
        in_specs=(
            P("filt", ("parts", "space"), None, None),
            P("filt", None, None),
            P("filt"),
            P("filt", ("parts", "space"), None, None),
        ),
        out_specs=(P("filt", ("parts", "space"), None, None), P(("parts", "filt"), None, None)),
        check_vma=False,
    )
```

```python
import jax
import jax.numpy as jnp
from jax import lax
from jax.sharding import PartitionSpec as P


def padded(block, sides, width):
    for axis, dim in sides:
        count = lax.axis_size(axis)
        forward = [(i, i + 1) for i in range(count - 1)]
        backward = [(target, source) for source, target in forward]
        low = lax.ppermute(
            lax.slice_in_dim(block, block.shape[dim] - width, None, axis=dim), axis, forward
        )
        high = lax.ppermute(lax.slice_in_dim(block, 0, width, axis=dim), axis, backward)
        block = jnp.concatenate([low, block, high], axis=dim)
    return block


def convolve(slab, kernel):
    return lax.conv_general_dilated(
        slab[None],
        kernel,
        (1, 1, 1),
        [(0, 0), (1, 1), (1, 1)],
        dimension_numbers=("NCDHW", "OIDHW", "NCDHW"),
        preferred_element_type=jnp.float32,
    )[0]


def plane_shifts(upstream):
    height = upstream.shape[2]
    length = upstream.shape[3]
    spread = jnp.pad(upstream, ((0, 0), (0, 0), (1, 1), (1, 1)))
    copies = []
    for tap in range(9):
        second = tap // 3
        third = tap % 3
        copies.append(
            spread[:, :, 2 - second : 2 - second + height, 2 - third : 2 - third + length]
        )
    stacked = jnp.stack(copies, 1)
    return stacked.reshape(upstream.shape[0] * 9, -1)


def tap_grads(rimmed, shifted, out_dev, depth):
    rows = []
    for first in range(3):
        window = lax.slice_in_dim(rimmed, first, first + depth, axis=1)
        flat = window.reshape(window.shape[0], -1)
        product = lax.dot_general(
            shifted, flat, (((1,), (1,)), ((), ())), preferred_element_type=jnp.float32
        )
        rows.append(product.reshape(out_dev, 9, window.shape[0]))
    return jnp.concatenate(rows, axis=1)


def space_sum(grads, beside=None, operand=None):
    count = lax.axis_size("space")
    if count != 4 or grads.shape[0] % 2:
        if beside is None:
            return lax.psum(grads, "space")
        return lax.psum(grads, "space"), beside(operand)
    core = lax.axis_index("space") % 2
    half = grads.shape[0] // 2
    pair = [(i, i ^ 1) for i in range(count)]
    across = [(i, i ^ 2) for i in range(count)]
    mine = lax.dynamic_slice_in_dim(grads, core * half, half, axis=0)
    other = lax.dynamic_slice_in_dim(grads, (1 - core) * half, half, axis=0)
    mine = mine + lax.ppermute(other, "space", pair)
    if beside is not None:
        mine, operand = lax.optimization_barrier((mine, operand))
    arrived = lax.ppermute(mine, "space", across)
    if beside is not None:
        result = beside(operand)
        arrived, result = lax.optimization_barrier((arrived, result))
    mine = mine + arrived
    theirs = lax.ppermute(mine, "space", pair)
    low = jnp.where(core == 0, mine, theirs)
    high = jnp.where(core == 0, theirs, mine)
    summed = jnp.concatenate([low, high], axis=0)
    if beside is None:
        return summed
    return summed, result


def on_device(volume, weight, bias, upstream):
    out_dev = weight.shape[0]
    in_all = weight.shape[2]
    in_dev = volume.shape[0]
    depth = upstream.shape[1]
    kernel = weight.reshape(out_dev, 3, 3, 3, in_all).transpose(0, 4, 1, 2, 3)
    shifted = plane_shifts(upstream)
    own = padded(volume, (("space", 1),), 1)
    own_grads = space_sum(tap_grads(own, shifted, out_dev, depth))
    whole = lax.all_gather(volume, "filt", axis=0, tiled=True)
    whole, own_grads = lax.optimization_barrier((whole, own_grads))
    rimmed = padded(whole, (("space", 1),), 1)
    start = lax.axis_index("filt") * in_dev
    rolled = jnp.roll(rimmed, -start, axis=0)
    rest = lax.slice_in_dim(rolled, in_dev, in_all, axis=0)

    def forward(slab):
        pre = convolve(slab, kernel) + bias[:, None, None, None]
        return jnp.where(pre > 0, pre, 0.3 * pre).astype(jnp.bfloat16)

    rest_grads, features = space_sum(tap_grads(rest, shifted, out_dev, depth), forward, rimmed)
    weight_grad = jnp.roll(jnp.concatenate([own_grads, rest_grads], axis=2), start, axis=2)
    return (features, weight_grad)


def solution(mesh):
    return jax.shard_map(
        on_device,
        mesh=mesh,
        in_specs=(
            P("filt", ("parts", "space"), None, None),
            P("filt", None, None),
            P("filt"),
            P("filt", ("parts", "space"), None, None),
        ),
        out_specs=(P("filt", ("parts", "space"), None, None), P(("parts", "filt"), None, None)),
        check_vma=False,
    )
```

```python
import jax
import jax.numpy as jnp
from jax import lax
from jax.sharding import PartitionSpec as P


def padded(block, sides, width):
    for axis, dim in sides:
        count = lax.axis_size(axis)
        forward = [(i, i + 1) for i in range(count - 1)]
        backward = [(target, source) for source, target in forward]
        low = lax.ppermute(
            lax.slice_in_dim(block, block.shape[dim] - width, None, axis=dim), axis, forward
        )
        high = lax.ppermute(lax.slice_in_dim(block, 0, width, axis=dim), axis, backward)
        block = jnp.concatenate([low, block, high], axis=dim)
    return block


def convolve(slab, kernel):
    return lax.conv_general_dilated(
        slab[None],
        kernel,
        (1, 1, 1),
        [(0, 0), (1, 1), (1, 1)],
        dimension_numbers=("NCDHW", "OIDHW", "NCDHW"),
        preferred_element_type=jnp.float32,
    )[0]


def plane_shifts(upstream):
    height = upstream.shape[2]
    length = upstream.shape[3]
    spread = jnp.pad(upstream, ((0, 0), (0, 0), (1, 1), (1, 1)))
    copies = []
    for tap in range(9):
        second = tap // 3
        third = tap % 3
        copies.append(
            spread[:, :, 2 - second : 2 - second + height, 2 - third : 2 - third + length]
        )
    stacked = jnp.stack(copies, 1)
    return stacked.reshape(upstream.shape[0] * 9, -1)


def tap_grads(rimmed, shifted, out_dev, depth):
    rows = []
    for first in range(3):
        window = lax.slice_in_dim(rimmed, first, first + depth, axis=1)
        flat = window.reshape(window.shape[0], -1)
        product = lax.dot_general(
            shifted, flat, (((1,), (1,)), ((), ())), preferred_element_type=jnp.float32
        )
        rows.append(product.reshape(out_dev, 9, window.shape[0]))
    return jnp.concatenate(rows, axis=1)


def line_gather(block, axis):
    count = lax.axis_size(axis)
    here = lax.axis_index(axis)
    lefts, rights = [], []
    from_left = block
    from_right = block
    for step in range(1, count):
        from_left = lax.ppermute(
            from_left, axis, [(i, i + 1) for i in range(step - 1, count - 1)]
        )
        from_right = lax.ppermute(
            from_right, axis, [(i, i - 1) for i in range(1, count - step + 1)]
        )
        lefts.append(from_left)
        rights.append(from_right)
    blocks = [block]
    for k in range(1, count):
        blocks.append(jnp.where(here + k < count, rights[k - 1], lefts[count - k - 1]))
    return jnp.concatenate(blocks, axis=0)


def space_sum(grads, beside=None, operand=None, tie=None):
    count = lax.axis_size("space")
    if count != 4 or grads.shape[0] % 2:
        if tie is not None:
            return lax.psum(grads, "space"), tie
        if beside is None:
            return lax.psum(grads, "space")
        return lax.psum(grads, "space"), beside(operand)
    core = lax.axis_index("space") % 2
    half = grads.shape[0] // 2
    pair = [(i, i ^ 1) for i in range(count)]
    across = [(i, i ^ 2) for i in range(count)]
    mine = lax.dynamic_slice_in_dim(grads, core * half, half, axis=0)
    other = lax.dynamic_slice_in_dim(grads, (1 - core) * half, half, axis=0)
    mine = mine + lax.ppermute(other, "space", pair)
    if tie is not None:
        mine, tie = lax.optimization_barrier((mine, tie))
    if beside is not None:
        mine, operand = lax.optimization_barrier((mine, operand))
    arrived = lax.ppermute(mine, "space", across)
    if beside is not None:
        result = beside(operand)
        arrived, result = lax.optimization_barrier((arrived, result))
    mine = mine + arrived
    theirs = lax.ppermute(mine, "space", pair)
    low = jnp.where(core == 0, mine, theirs)
    high = jnp.where(core == 0, theirs, mine)
    summed = jnp.concatenate([low, high], axis=0)
    if tie is not None:
        return summed, tie
    if beside is None:
        return summed
    return summed, result


def on_device(volume, weight, bias, upstream):
    out_dev = weight.shape[0]
    in_all = weight.shape[2]
    in_dev = volume.shape[0]
    depth = upstream.shape[1]
    kernel = weight.reshape(out_dev, 3, 3, 3, in_all).transpose(0, 4, 1, 2, 3)
    shifted = plane_shifts(upstream)
    own = padded(volume, (("space", 1),), 1)
    rolled = line_gather(volume, "filt")
    own_grads, rolled = space_sum(tap_grads(own, shifted, out_dev, depth), tie=rolled)
    rolled = padded(rolled, (("space", 1),), 1)
    start = lax.axis_index("filt") * in_dev
    rimmed = jnp.roll(rolled, start, axis=0)
    rest = lax.slice_in_dim(rolled, in_dev, in_all, axis=0)

    def forward(slab):
        pre = convolve(slab, kernel) + bias[:, None, None, None]
        return jnp.where(pre > 0, pre, 0.3 * pre).astype(jnp.bfloat16)

    rest_grads, features = space_sum(tap_grads(rest, shifted, out_dev, depth), forward, rimmed)
    weight_grad = jnp.roll(jnp.concatenate([own_grads, rest_grads], axis=2), start, axis=2)
    return (features, weight_grad)


def solution(mesh):
    return jax.shard_map(
        on_device,
        mesh=mesh,
        in_specs=(
            P("filt", ("parts", "space"), None, None),
            P("filt", None, None),
            P("filt"),
            P("filt", ("parts", "space"), None, None),
        ),
        out_specs=(P("filt", ("parts", "space"), None, None), P(("parts", "filt"), None, None)),
        check_vma=False,
    )
```

```python
import jax
import jax.numpy as jnp
from jax import lax
from jax.sharding import PartitionSpec as P


def padded(block, sides, width):
    for axis, dim in sides:
        count = lax.axis_size(axis)
        forward = [(i, i + 1) for i in range(count - 1)]
        backward = [(target, source) for source, target in forward]
        low = lax.ppermute(
            lax.slice_in_dim(block, block.shape[dim] - width, None, axis=dim), axis, forward
        )
        high = lax.ppermute(lax.slice_in_dim(block, 0, width, axis=dim), axis, backward)
        block = jnp.concatenate([low, block, high], axis=dim)
    return block


def convolve(slab, kernel):
    return lax.conv_general_dilated(
        slab[None],
        kernel,
        (1, 1, 1),
        [(0, 0), (1, 1), (1, 1)],
        dimension_numbers=("NCDHW", "OIDHW", "NCDHW"),
        preferred_element_type=jnp.float32,
    )[0]


def plane_shifts(upstream):
    height = upstream.shape[2]
    length = upstream.shape[3]
    spread = jnp.pad(upstream, ((0, 0), (0, 0), (1, 1), (1, 1)))
    copies = []
    for tap in range(9):
        second = tap // 3
        third = tap % 3
        copies.append(
            spread[:, :, 2 - second : 2 - second + height, 2 - third : 2 - third + length]
        )
    stacked = jnp.stack(copies, 1)
    return stacked.reshape(upstream.shape[0] * 9, -1)


def tap_grads(rimmed, shifted, out_dev, depth):
    rows = []
    for first in range(3):
        window = lax.slice_in_dim(rimmed, first, first + depth, axis=1)
        flat = window.reshape(window.shape[0], -1)
        product = lax.dot_general(
            shifted, flat, (((1,), (1,)), ((), ())), preferred_element_type=jnp.float32
        )
        rows.append(product.reshape(out_dev, 9, window.shape[0]))
    return jnp.concatenate(rows, axis=1)


def line_gather(block, axis):
    count = lax.axis_size(axis)
    here = lax.axis_index(axis)
    lefts, rights = line_steps(block, axis)
    blocks = [block]
    for k in range(1, count):
        blocks.append(jnp.where(here + k < count, rights[k - 1], lefts[count - k - 1]))
    return jnp.concatenate(blocks, axis=0)


def stacked_grads(rimmed, shifted, out_dev, depth):
    windows = [lax.slice_in_dim(rimmed, first, first + depth, axis=1) for first in range(3)]
    flat = jnp.concatenate(windows, axis=0).reshape(3 * rimmed.shape[0], -1)
    product = lax.dot_general(
        shifted, flat, (((1,), (1,)), ((), ())), preferred_element_type=jnp.float32
    )
    product = product.reshape(out_dev, 9, 3, rimmed.shape[0]).transpose(0, 2, 1, 3)
    return product.reshape(out_dev, 27, rimmed.shape[0])


def line_steps(block, axis):
    count = lax.axis_size(axis)
    lefts, rights = [], []
    from_left = block
    from_right = block
    for step in range(1, count):
        from_left = lax.ppermute(
            from_left, axis, [(i, i + 1) for i in range(step - 1, count - 1)]
        )
        from_right = lax.ppermute(
            from_right, axis, [(i, i - 1) for i in range(1, count - step + 1)]
        )
        lefts.append(from_left)
        rights.append(from_right)
    return lefts, rights


def halves(grads):
    core = lax.axis_index("space") % 2
    half = grads.shape[0] // 2
    mine = lax.dynamic_slice_in_dim(grads, core * half, half, axis=0)
    other = lax.dynamic_slice_in_dim(grads, (1 - core) * half, half, axis=0)
    pair = [(i, i ^ 1) for i in range(4)]
    return mine + lax.ppermute(other, "space", pair)


def finish(mine, arrived):
    core = lax.axis_index("space") % 2
    pair = [(i, i ^ 1) for i in range(4)]
    mine = mine + arrived
    theirs = lax.ppermute(mine, "space", pair)
    low = jnp.where(core == 0, mine, theirs)
    high = jnp.where(core == 0, theirs, mine)
    return jnp.concatenate([low, high], axis=0)


def ranked(volume, weight, bias, upstream):
    out_dev = weight.shape[0]
    in_all = weight.shape[2]
    in_dev = volume.shape[0]
    depth = upstream.shape[1]
    kernel = weight.reshape(out_dev, 3, 3, 3, in_all).transpose(0, 4, 1, 2, 3)
    shifted = plane_shifts(upstream)
    here = lax.axis_index("filt")
    across = [(i, i ^ 2) for i in range(4)]
    lefts, rights = line_steps(volume, "filt")
    blocks = [
        volume,
        jnp.where(here == 0, rights[0], lefts[0]),
        jnp.where(here == 0, rights[1], jnp.where(here == 3, lefts[1], rights[0])),
        jnp.where(
            here == 0, rights[2], jnp.where(here == 1, rights[1], jnp.where(here == 2, lefts[1], lefts[2]))
        ),
    ]
    places = [
        here,
        jnp.where(here == 0, 1, here - 1),
        jnp.where(here == 0, 2, jnp.where(here == 3, 1, here + 1)),
        jnp.where(here <= 1, 3, 0),
    ]
    rims = []
    sums = []
    prior = None
    arrived = None
    features = None
    for j, block in enumerate(blocks):
        if prior is not None:
            block, prior = lax.optimization_barrier((block, prior))
        rim = padded(block, (("space", 1),), 1)
        rims.append(rim)
        mine = halves(stacked_grads(rim, shifted, out_dev, depth))
        if arrived is not None:
            mine, arrived = lax.optimization_barrier((mine, arrived))
            sums.append(finish(prior, arrived))
        if j == len(blocks) - 1:
            whole = jnp.zeros((in_all,) + rim.shape[1:], rim.dtype)
            for part, place in zip(rims, places):
                whole = lax.dynamic_update_slice_in_dim(whole, part, place * in_dev, axis=0)
            mine, whole = lax.optimization_barrier((mine, whole))
        prior = mine
        arrived = lax.ppermute(mine, "space", across)
        if j == len(blocks) - 1:
            pre = convolve(whole, kernel) + bias[:, None, None, None]
            features = jnp.where(pre > 0, pre, 0.3 * pre).astype(jnp.bfloat16)
            arrived, features = lax.optimization_barrier((arrived, features))
    sums.append(finish(prior, arrived))
    weight_grad = jnp.zeros((out_dev, 27, in_all), jnp.float32)
    for part, place in zip(sums, places):
        weight_grad = lax.dynamic_update_slice_in_dim(weight_grad, part, place * in_dev, axis=2)
    return (features, weight_grad)


def space_sum(grads, beside=None, operand=None, tie=None):
    count = lax.axis_size("space")
    if count != 4 or grads.shape[0] % 2:
        if tie is not None:
            return lax.psum(grads, "space"), tie
        if beside is None:
            return lax.psum(grads, "space")
        return lax.psum(grads, "space"), beside(operand)
    core = lax.axis_index("space") % 2
    half = grads.shape[0] // 2
    pair = [(i, i ^ 1) for i in range(count)]
    across = [(i, i ^ 2) for i in range(count)]
    mine = lax.dynamic_slice_in_dim(grads, core * half, half, axis=0)
    other = lax.dynamic_slice_in_dim(grads, (1 - core) * half, half, axis=0)
    mine = mine + lax.ppermute(other, "space", pair)
    if tie is not None:
        mine, tie = lax.optimization_barrier((mine, tie))
    if beside is not None:
        mine, operand = lax.optimization_barrier((mine, operand))
    arrived = lax.ppermute(mine, "space", across)
    if beside is not None:
        result = beside(operand)
        arrived, result = lax.optimization_barrier((arrived, result))
    mine = mine + arrived
    theirs = lax.ppermute(mine, "space", pair)
    low = jnp.where(core == 0, mine, theirs)
    high = jnp.where(core == 0, theirs, mine)
    summed = jnp.concatenate([low, high], axis=0)
    if tie is not None:
        return summed, tie
    if beside is None:
        return summed
    return summed, result


def on_device(volume, weight, bias, upstream):
    if lax.axis_size("filt") == 4 and lax.axis_size("space") == 4 and weight.shape[0] % 2 == 0:
        return ranked(volume, weight, bias, upstream)
    out_dev = weight.shape[0]
    in_all = weight.shape[2]
    in_dev = volume.shape[0]
    depth = upstream.shape[1]
    kernel = weight.reshape(out_dev, 3, 3, 3, in_all).transpose(0, 4, 1, 2, 3)
    shifted = plane_shifts(upstream)
    own = padded(volume, (("space", 1),), 1)
    rolled = line_gather(volume, "filt")
    own_grads, rolled = space_sum(tap_grads(own, shifted, out_dev, depth), tie=rolled)
    rolled = padded(rolled, (("space", 1),), 1)
    start = lax.axis_index("filt") * in_dev
    rimmed = jnp.roll(rolled, start, axis=0)
    rest = lax.slice_in_dim(rolled, in_dev, in_all, axis=0)

    def forward(slab):
        pre = convolve(slab, kernel) + bias[:, None, None, None]
        return jnp.where(pre > 0, pre, 0.3 * pre).astype(jnp.bfloat16)

    rest_grads, features = space_sum(tap_grads(rest, shifted, out_dev, depth), forward, rimmed)
    weight_grad = jnp.roll(jnp.concatenate([own_grads, rest_grads], axis=2), start, axis=2)
    return (features, weight_grad)


def solution(mesh):
    return jax.shard_map(
        on_device,
        mesh=mesh,
        in_specs=(
            P("filt", ("parts", "space"), None, None),
            P("filt", None, None),
            P("filt"),
            P("filt", ("parts", "space"), None, None),
        ),
        out_specs=(P("filt", ("parts", "space"), None, None), P(("parts", "filt"), None, None)),
        check_vma=False,
    )
```

```python
import jax
import jax.numpy as jnp
from jax import lax
from jax.sharding import PartitionSpec as P


def padded(block, sides, width):
    for axis, dim in sides:
        count = lax.axis_size(axis)
        forward = [(i, i + 1) for i in range(count - 1)]
        backward = [(target, source) for source, target in forward]
        low = lax.ppermute(
            lax.slice_in_dim(block, block.shape[dim] - width, None, axis=dim), axis, forward
        )
        high = lax.ppermute(lax.slice_in_dim(block, 0, width, axis=dim), axis, backward)
        block = jnp.concatenate([low, block, high], axis=dim)
    return block


def convolve(slab, kernel):
    return lax.conv_general_dilated(
        slab[None],
        kernel,
        (1, 1, 1),
        [(0, 0), (1, 1), (1, 1)],
        dimension_numbers=("NCDHW", "OIDHW", "NCDHW"),
        preferred_element_type=jnp.float32,
    )[0]


def plane_shifts(upstream):
    height = upstream.shape[2]
    length = upstream.shape[3]
    spread = jnp.pad(upstream, ((0, 0), (0, 0), (1, 1), (1, 1)))
    copies = []
    for tap in range(9):
        second = tap // 3
        third = tap % 3
        copies.append(
            spread[:, :, 2 - second : 2 - second + height, 2 - third : 2 - third + length]
        )
    stacked = jnp.stack(copies, 1)
    return stacked.reshape(upstream.shape[0] * 9, -1)


def tap_grads(rimmed, shifted, out_dev, depth):
    rows = []
    for first in range(3):
        window = lax.slice_in_dim(rimmed, first, first + depth, axis=1)
        flat = window.reshape(window.shape[0], -1)
        product = lax.dot_general(
            shifted, flat, (((1,), (1,)), ((), ())), preferred_element_type=jnp.float32
        )
        rows.append(product.reshape(out_dev, 9, window.shape[0]))
    return jnp.concatenate(rows, axis=1)


def line_gather(block, axis):
    count = lax.axis_size(axis)
    here = lax.axis_index(axis)
    lefts, rights = [], []
    from_left = block
    from_right = block
    for step in range(1, count):
        from_left = lax.ppermute(
            from_left, axis, [(i, i + 1) for i in range(step - 1, count - 1)]
        )
        from_right = lax.ppermute(
            from_right, axis, [(i, i - 1) for i in range(1, count - step + 1)]
        )
        lefts.append(from_left)
        rights.append(from_right)
    blocks = [block]
    for k in range(1, count):
        blocks.append(jnp.where(here + k < count, rights[k - 1], lefts[count - k - 1]))
    return jnp.concatenate(blocks, axis=0)


def space_sum(grads, beside=None, operand=None, tie=None):
    count = lax.axis_size("space")
    if count != 4 or grads.shape[0] % 2:
        summed = lax.psum(grads, "space")
        if tie is not None:
            return summed, tie
        if beside is None:
            return summed
        return summed, beside(operand)
    chip = lax.axis_index("space") // 2
    half = grads.shape[0] // 2
    pair = [(i, i ^ 1) for i in range(count)]
    across = [(i, i ^ 2) for i in range(count)]
    keep = lax.dynamic_slice_in_dim(grads, chip * half, half, axis=0)
    send = lax.dynamic_slice_in_dim(grads, (1 - chip) * half, half, axis=0)
    arrived = lax.ppermute(send, "space", across)
    if beside is not None:
        result = beside(operand)
        arrived, result = lax.optimization_barrier((arrived, result))
    mine = keep + arrived
    mine = mine + lax.ppermute(mine, "space", pair)
    theirs = lax.ppermute(mine, "space", across)
    low = jnp.where(chip == 0, mine, theirs)
    high = jnp.where(chip == 0, theirs, mine)
    summed = jnp.concatenate([low, high], axis=0)
    if tie is not None:
        summed, tie = lax.optimization_barrier((summed, tie))
        return summed, tie
    if beside is None:
        return summed
    return summed, result


def on_device(volume, weight, bias, upstream):
    out_dev = weight.shape[0]
    in_all = weight.shape[2]
    in_dev = volume.shape[0]
    depth = upstream.shape[1]
    kernel = weight.reshape(out_dev, 3, 3, 3, in_all).transpose(0, 4, 1, 2, 3)
    shifted = plane_shifts(upstream)
    own = padded(volume, (("space", 1),), 1)
    rolled = line_gather(volume, "filt")
    own_grads, rolled = space_sum(tap_grads(own, shifted, out_dev, depth), tie=rolled)
    rolled = padded(rolled, (("space", 1),), 1)
    start = lax.axis_index("filt") * in_dev
    rimmed = jnp.roll(rolled, start, axis=0)
    rest = lax.slice_in_dim(rolled, in_dev, in_all, axis=0)

    def forward(slab):
        pre = convolve(slab, kernel) + bias[:, None, None, None]
        return jnp.where(pre > 0, pre, 0.3 * pre).astype(jnp.bfloat16)

    rest_grads, features = space_sum(tap_grads(rest, shifted, out_dev, depth), forward, rimmed)
    weight_grad = jnp.roll(jnp.concatenate([own_grads, rest_grads], axis=2), start, axis=2)
    return (features, weight_grad)


def solution(mesh):
    return jax.shard_map(
        on_device,
        mesh=mesh,
        in_specs=(
            P("filt", ("parts", "space"), None, None),
            P("filt", None, None),
            P("filt"),
            P("filt", ("parts", "space"), None, None),
        ),
        out_specs=(P("filt", ("parts", "space"), None, None), P(("parts", "filt"), None, None)),
        check_vma=False,
    )
```

```python
import jax
import jax.numpy as jnp
from jax import lax
from jax.sharding import PartitionSpec as P


def padded(block, sides, width):
    for axis, dim in sides:
        count = lax.axis_size(axis)
        forward = [(i, i + 1) for i in range(count - 1)]
        backward = [(target, source) for source, target in forward]
        low = lax.ppermute(
            lax.slice_in_dim(block, block.shape[dim] - width, None, axis=dim), axis, forward
        )
        high = lax.ppermute(lax.slice_in_dim(block, 0, width, axis=dim), axis, backward)
        block = jnp.concatenate([low, block, high], axis=dim)
    return block


def convolve(slab, kernel):
    return lax.conv_general_dilated(
        slab[None],
        kernel,
        (1, 1, 1),
        [(0, 0), (1, 1), (1, 1)],
        dimension_numbers=("NCDHW", "OIDHW", "NCDHW"),
        preferred_element_type=jnp.float32,
    )[0]


def plane_shifts(upstream):
    height = upstream.shape[2]
    length = upstream.shape[3]
    spread = jnp.pad(upstream, ((0, 0), (0, 0), (1, 1), (1, 1)))
    copies = []
    for tap in range(9):
        second = tap // 3
        third = tap % 3
        copies.append(
            spread[:, :, 2 - second : 2 - second + height, 2 - third : 2 - third + length]
        )
    stacked = jnp.stack(copies, 1)
    return stacked.reshape(upstream.shape[0] * 9, -1)


def tap_grads(rimmed, shifted, out_dev, depth):
    rows = []
    for first in range(3):
        window = lax.slice_in_dim(rimmed, first, first + depth, axis=1)
        flat = window.reshape(window.shape[0], -1)
        product = lax.dot_general(
            shifted, flat, (((1,), (1,)), ((), ())), preferred_element_type=jnp.float32
        )
        rows.append(product.reshape(out_dev, 9, window.shape[0]))
    return jnp.concatenate(rows, axis=1)


def line_gather(block, axis):
    count = lax.axis_size(axis)
    here = lax.axis_index(axis)
    lefts, rights = [], []
    from_left = block
    from_right = block
    for step in range(1, count):
        from_left = lax.ppermute(
            from_left, axis, [(i, i + 1) for i in range(step - 1, count - 1)]
        )
        from_right = lax.ppermute(
            from_right, axis, [(i, i - 1) for i in range(1, count - step + 1)]
        )
        lefts.append(from_left)
        rights.append(from_right)
    blocks = [block]
    for k in range(1, count):
        blocks.append(jnp.where(here + k < count, rights[k - 1], lefts[count - k - 1]))
    return jnp.concatenate(blocks, axis=0)


def space_sum(grads, beside=None, operand=None, tie=None):
    count = lax.axis_size("space")
    if count != 4 or grads.shape[0] % 2:
        if tie is not None:
            return lax.psum(grads, "space"), tie
        if beside is None:
            return lax.psum(grads, "space")
        return lax.psum(grads, "space"), beside(operand)
    core = lax.axis_index("space") % 2
    half = grads.shape[0] // 2
    pair = [(i, i ^ 1) for i in range(count)]
    across = [(i, i ^ 2) for i in range(count)]
    mine = lax.dynamic_slice_in_dim(grads, core * half, half, axis=0)
    other = lax.dynamic_slice_in_dim(grads, (1 - core) * half, half, axis=0)
    mine = mine + lax.ppermute(other, "space", pair)
    if beside is not None:
        mine, operand = lax.optimization_barrier((mine, operand))
    arrived = lax.ppermute(mine, "space", across)
    if beside is not None:
        result = beside(operand)
        arrived, result = lax.optimization_barrier((arrived, result))
    mine = mine + arrived
    theirs = lax.ppermute(mine, "space", pair)
    low = jnp.where(core == 0, mine, theirs)
    high = jnp.where(core == 0, theirs, mine)
    summed = jnp.concatenate([low, high], axis=0)
    if tie is not None:
        return lax.optimization_barrier((summed, tie))
    if beside is None:
        return summed
    return summed, result


def on_device(volume, weight, bias, upstream):
    out_dev = weight.shape[0]
    in_all = weight.shape[2]
    in_dev = volume.shape[0]
    depth = upstream.shape[1]
    kernel = weight.reshape(out_dev, 3, 3, 3, in_all).transpose(0, 4, 1, 2, 3)
    shifted = plane_shifts(upstream)
    own = padded(volume, (("space", 1),), 1)
    rolled = line_gather(volume, "filt")
    own_grads, rolled = space_sum(tap_grads(own, shifted, out_dev, depth), tie=rolled)
    rolled = padded(rolled, (("space", 1),), 1)
    start = lax.axis_index("filt") * in_dev
    rimmed = jnp.roll(rolled, start, axis=0)
    rest = lax.slice_in_dim(rolled, in_dev, in_all, axis=0)

    def forward(slab):
        pre = convolve(slab, kernel) + bias[:, None, None, None]
        return jnp.where(pre > 0, pre, 0.3 * pre).astype(jnp.bfloat16)

    rest_grads, features = space_sum(tap_grads(rest, shifted, out_dev, depth), forward, rimmed)
    weight_grad = jnp.roll(jnp.concatenate([own_grads, rest_grads], axis=2), start, axis=2)
    return (features, weight_grad)


def solution(mesh):
    return jax.shard_map(
        on_device,
        mesh=mesh,
        in_specs=(
            P("filt", ("parts", "space"), None, None),
            P("filt", None, None),
            P("filt"),
            P("filt", ("parts", "space"), None, None),
        ),
        out_specs=(P("filt", ("parts", "space"), None, None), P(("parts", "filt"), None, None)),
        check_vma=False,
    )
```

```python
import jax
import jax.numpy as jnp
from jax import lax
from jax.sharding import PartitionSpec as P


def padded(block, sides, width):
    for axis, dim in sides:
        count = lax.axis_size(axis)
        forward = [(i, i + 1) for i in range(count - 1)]
        backward = [(target, source) for source, target in forward]
        low = lax.ppermute(
            lax.slice_in_dim(block, block.shape[dim] - width, None, axis=dim), axis, forward
        )
        high = lax.ppermute(lax.slice_in_dim(block, 0, width, axis=dim), axis, backward)
        block = jnp.concatenate([low, block, high], axis=dim)
    return block


def convolve(slab, kernel):
    return lax.conv_general_dilated(
        slab[None],
        kernel,
        (1, 1, 1),
        [(0, 0), (1, 1), (1, 1)],
        dimension_numbers=("NCDHW", "OIDHW", "NCDHW"),
        preferred_element_type=jnp.float32,
    )[0]


def plane_shifts(upstream):
    height = upstream.shape[2]
    length = upstream.shape[3]
    spread = jnp.pad(upstream, ((0, 0), (0, 0), (1, 1), (1, 1)))
    copies = []
    for tap in range(9):
        second = tap // 3
        third = tap % 3
        copies.append(
            spread[:, :, 2 - second : 2 - second + height, 2 - third : 2 - third + length]
        )
    stacked = jnp.stack(copies, 1)
    return stacked.reshape(upstream.shape[0] * 9, -1)


def tap_grads(rimmed, shifted, out_dev, depth):
    rows = []
    for first in range(3):
        window = lax.slice_in_dim(rimmed, first, first + depth, axis=1)
        flat = window.reshape(window.shape[0], -1)
        product = lax.dot_general(
            shifted, flat, (((1,), (1,)), ((), ())), preferred_element_type=jnp.float32
        )
        rows.append(product.reshape(out_dev, 9, window.shape[0]))
    return jnp.concatenate(rows, axis=1)


def line_steps(block, axis):
    count = lax.axis_size(axis)
    lefts, rights = [], []
    from_left = block
    from_right = block
    for step in range(1, count):
        from_left = lax.ppermute(
            from_left, axis, [(i, i + 1) for i in range(step - 1, count - 1)]
        )
        from_right = lax.ppermute(
            from_right, axis, [(i, i - 1) for i in range(1, count - step + 1)]
        )
        lefts.append(from_left)
        rights.append(from_right)
    return lefts, rights


def line_gather(block, axis, lefts, rights):
    count = lax.axis_size(axis)
    here = lax.axis_index(axis)
    blocks = [block]
    for k in range(1, count):
        blocks.append(jnp.where(here + k < count, rights[k - 1], lefts[count - k - 1]))
    return jnp.concatenate(blocks, axis=0)


def space_sum(grads, beside=None, operand=None, tie=None, early=None):
    count = lax.axis_size("space")
    if count != 4 or grads.shape[0] % 2:
        if tie is not None:
            return lax.psum(grads, "space"), tie
        if beside is None:
            return lax.psum(grads, "space")
        return lax.psum(grads, "space"), beside(operand)
    core = lax.axis_index("space") % 2
    half = grads.shape[0] // 2
    pair = [(i, i ^ 1) for i in range(count)]
    across = [(i, i ^ 2) for i in range(count)]
    mine = lax.dynamic_slice_in_dim(grads, core * half, half, axis=0)
    other = lax.dynamic_slice_in_dim(grads, (1 - core) * half, half, axis=0)
    mine = mine + lax.ppermute(other, "space", pair)
    if early is not None:
        mine, early = lax.optimization_barrier((mine, early))
    if beside is not None:
        mine, operand = lax.optimization_barrier((mine, operand))
    arrived = lax.ppermute(mine, "space", across)
    if beside is not None:
        result = beside(operand)
        arrived, result = lax.optimization_barrier((arrived, result))
    mine = mine + arrived
    theirs = lax.ppermute(mine, "space", pair)
    low = jnp.where(core == 0, mine, theirs)
    high = jnp.where(core == 0, theirs, mine)
    summed = jnp.concatenate([low, high], axis=0)
    if tie is not None:
        return lax.optimization_barrier((summed, tie))
    if beside is None:
        return summed
    return summed, result


def on_device(volume, weight, bias, upstream):
    out_dev = weight.shape[0]
    in_all = weight.shape[2]
    in_dev = volume.shape[0]
    depth = upstream.shape[1]
    kernel = weight.reshape(out_dev, 3, 3, 3, in_all).transpose(0, 4, 1, 2, 3)
    shifted = plane_shifts(upstream)
    lefts, rights = line_steps(volume, "filt")
    own = padded(volume, (("space", 1),), 1)
    if len(lefts) > 1:
        own, lefts[0], rights[0] = lax.optimization_barrier((own, lefts[0], rights[0]))
        early = (lefts[1], rights[1])
    else:
        early = None
    own_grads = tap_grads(own, shifted, out_dev, depth)
    rolled = line_gather(volume, "filt", lefts, rights)
    own_grads, rolled = space_sum(own_grads, tie=rolled, early=early)
    rolled = padded(rolled, (("space", 1),), 1)
    start = lax.axis_index("filt") * in_dev
    rimmed = jnp.roll(rolled, start, axis=0)
    rest = lax.slice_in_dim(rolled, in_dev, in_all, axis=0)

    def forward(slab):
        pre = convolve(slab, kernel) + bias[:, None, None, None]
        return jnp.where(pre > 0, pre, 0.3 * pre).astype(jnp.bfloat16)

    rest_grads, features = space_sum(tap_grads(rest, shifted, out_dev, depth), forward, rimmed)
    weight_grad = jnp.roll(jnp.concatenate([own_grads, rest_grads], axis=2), start, axis=2)
    return (features, weight_grad)


def solution(mesh):
    return jax.shard_map(
        on_device,
        mesh=mesh,
        in_specs=(
            P("filt", ("parts", "space"), None, None),
            P("filt", None, None),
            P("filt"),
            P("filt", ("parts", "space"), None, None),
        ),
        out_specs=(P("filt", ("parts", "space"), None, None), P(("parts", "filt"), None, None)),
        check_vma=False,
    )
```

```python
import jax
import jax.numpy as jnp
from jax import lax
from jax.sharding import PartitionSpec as P


def padded(block, sides, width):
    for axis, dim in sides:
        count = lax.axis_size(axis)
        forward = [(i, i + 1) for i in range(count - 1)]
        backward = [(target, source) for source, target in forward]
        low = lax.ppermute(
            lax.slice_in_dim(block, block.shape[dim] - width, None, axis=dim), axis, forward
        )
        high = lax.ppermute(lax.slice_in_dim(block, 0, width, axis=dim), axis, backward)
        block = jnp.concatenate([low, block, high], axis=dim)
    return block


def convolve(slab, kernel):
    return lax.conv_general_dilated(
        slab[None],
        kernel,
        (1, 1, 1),
        [(0, 0), (1, 1), (1, 1)],
        dimension_numbers=("NCDHW", "OIDHW", "NCDHW"),
        preferred_element_type=jnp.float32,
    )[0]


def plane_shifts(upstream):
    height = upstream.shape[2]
    length = upstream.shape[3]
    spread = jnp.pad(upstream, ((0, 0), (0, 0), (1, 1), (1, 1)))
    copies = []
    for tap in range(9):
        second = tap // 3
        third = tap % 3
        copies.append(
            spread[:, :, 2 - second : 2 - second + height, 2 - third : 2 - third + length]
        )
    stacked = jnp.stack(copies, 1)
    return stacked.reshape(upstream.shape[0] * 9, -1)


def tap_grads(rimmed, shifted, out_dev, depth):
    rows = []
    for first in range(3):
        window = lax.slice_in_dim(rimmed, first, first + depth, axis=1)
        flat = window.reshape(window.shape[0], -1)
        product = lax.dot_general(
            shifted, flat, (((1,), (1,)), ((), ())), preferred_element_type=jnp.float32
        )
        rows.append(product.reshape(out_dev, 9, window.shape[0]))
    return jnp.concatenate(rows, axis=1)


def line_steps(block, axis):
    count = lax.axis_size(axis)
    lefts, rights = [], []
    from_left = block
    from_right = block
    for step in range(1, count):
        from_left = lax.ppermute(
            from_left, axis, [(i, i + 1) for i in range(step - 1, count - 1)]
        )
        from_right = lax.ppermute(
            from_right, axis, [(i, i - 1) for i in range(1, count - step + 1)]
        )
        lefts.append(from_left)
        rights.append(from_right)
    return lefts, rights


def line_gather(block, axis, lefts, rights):
    count = lax.axis_size(axis)
    here = lax.axis_index(axis)
    blocks = [block]
    for k in range(1, count):
        blocks.append(jnp.where(here + k < count, rights[k - 1], lefts[count - k - 1]))
    return jnp.concatenate(blocks, axis=0)


def space_sum(grads, beside=None, operand=None, early=None):
    count = lax.axis_size("space")
    result = None
    if count != 4 or grads.shape[0] % 2:
        if beside is not None:
            result = beside(operand)
        return lax.psum(grads, "space"), result, early
    core = lax.axis_index("space") % 2
    half = grads.shape[0] // 2
    pair = [(i, i ^ 1) for i in range(count)]
    across = [(i, i ^ 2) for i in range(count)]
    mine = lax.dynamic_slice_in_dim(grads, core * half, half, axis=0)
    other = lax.dynamic_slice_in_dim(grads, (1 - core) * half, half, axis=0)
    mine = mine + lax.ppermute(other, "space", pair)
    if early is not None:
        mine, early = lax.optimization_barrier((mine, early))
    if beside is not None:
        mine, operand = lax.optimization_barrier((mine, operand))
    arrived = lax.ppermute(mine, "space", across)
    if beside is not None:
        result = beside(operand)
        arrived, result = lax.optimization_barrier((arrived, result))
    mine = mine + arrived
    theirs = lax.ppermute(mine, "space", pair)
    low = jnp.where(core == 0, mine, theirs)
    high = jnp.where(core == 0, theirs, mine)
    return jnp.concatenate([low, high], axis=0), result, early


def on_device(volume, weight, bias, upstream):
    out_dev = weight.shape[0]
    in_all = weight.shape[2]
    in_dev = volume.shape[0]
    depth = upstream.shape[1]
    kernel = weight.reshape(out_dev, 3, 3, 3, in_all).transpose(0, 4, 1, 2, 3)
    shifted = plane_shifts(upstream)
    lefts, rights = line_steps(volume, "filt")
    own = padded(volume, (("space", 1),), 1)
    first = min(2, len(lefts))
    tied = lax.optimization_barrier((own, lefts[:first], rights[:first]))
    own, lefts[:first], rights[:first] = tied
    later = (lefts[first:], rights[first:])
    own_grads, _, later = space_sum(tap_grads(own, shifted, out_dev, depth), early=later)
    lefts[first:], rights[first:] = later
    rolled = line_gather(volume, "filt", lefts, rights)
    rolled = padded(rolled, (("space", 1),), 1)
    start = lax.axis_index("filt") * in_dev
    rimmed = jnp.roll(rolled, start, axis=0)
    rest = lax.slice_in_dim(rolled, in_dev, in_all, axis=0)

    def forward(slab):
        pre = convolve(slab, kernel) + bias[:, None, None, None]
        return jnp.where(pre > 0, pre, 0.3 * pre).astype(jnp.bfloat16)

    rest_grads, features, own_grads = space_sum(
        tap_grads(rest, shifted, out_dev, depth), forward, rimmed, early=own_grads
    )
    weight_grad = jnp.roll(jnp.concatenate([own_grads, rest_grads], axis=2), start, axis=2)
    return (features, weight_grad)


def solution(mesh):
    return jax.shard_map(
        on_device,
        mesh=mesh,
        in_specs=(
            P("filt", ("parts", "space"), None, None),
            P("filt", None, None),
            P("filt"),
            P("filt", ("parts", "space"), None, None),
        ),
        out_specs=(P("filt", ("parts", "space"), None, None), P(("parts", "filt"), None, None)),
        check_vma=False,
    )
```

```python
import jax
import jax.numpy as jnp
from jax import lax
from jax.sharding import PartitionSpec as P


def padded(block, sides, width):
    for axis, dim in sides:
        count = lax.axis_size(axis)
        forward = [(i, i + 1) for i in range(count - 1)]
        backward = [(target, source) for source, target in forward]
        low = lax.ppermute(
            lax.slice_in_dim(block, block.shape[dim] - width, None, axis=dim), axis, forward
        )
        high = lax.ppermute(lax.slice_in_dim(block, 0, width, axis=dim), axis, backward)
        block = jnp.concatenate([low, block, high], axis=dim)
    return block


def convolve(slab, kernel):
    return lax.conv_general_dilated(
        slab[None],
        kernel,
        (1, 1, 1),
        [(0, 0), (1, 1), (1, 1)],
        dimension_numbers=("NCDHW", "OIDHW", "NCDHW"),
        preferred_element_type=jnp.float32,
    )[0]


def plane_shifts(upstream):
    height = upstream.shape[2]
    length = upstream.shape[3]
    spread = jnp.pad(upstream, ((0, 0), (0, 0), (1, 1), (1, 1)))
    copies = []
    for tap in range(9):
        second = tap // 3
        third = tap % 3
        copies.append(
            spread[:, :, 2 - second : 2 - second + height, 2 - third : 2 - third + length]
        )
    stacked = jnp.stack(copies, 1)
    return stacked.reshape(upstream.shape[0] * 9, -1)


def tap_grads(rimmed, shifted, out_dev, depth):
    rows = []
    for first in range(3):
        window = lax.slice_in_dim(rimmed, first, first + depth, axis=1)
        flat = window.reshape(window.shape[0], -1)
        product = lax.dot_general(
            shifted, flat, (((1,), (1,)), ((), ())), preferred_element_type=jnp.float32
        )
        rows.append(product.reshape(out_dev, 9, window.shape[0]))
    return jnp.concatenate(rows, axis=1)


def line_steps(block, axis):
    count = lax.axis_size(axis)
    lefts, rights = [], []
    from_left = block
    from_right = block
    for step in range(1, count):
        from_left = lax.ppermute(
            from_left, axis, [(i, i + 1) for i in range(step - 1, count - 1)]
        )
        from_right = lax.ppermute(
            from_right, axis, [(i, i - 1) for i in range(1, count - step + 1)]
        )
        lefts.append(from_left)
        rights.append(from_right)
    return lefts, rights


def line_gather(block, axis, lefts, rights):
    count = lax.axis_size(axis)
    here = lax.axis_index(axis)
    blocks = [block]
    for k in range(1, count):
        blocks.append(jnp.where(here + k < count, rights[k - 1], lefts[count - k - 1]))
    return jnp.concatenate(blocks, axis=0)


def space_sum(grads, beside=None, operand=None, early=None):
    count = lax.axis_size("space")
    result = None
    if count != 4 or grads.shape[0] % 2:
        if beside is not None:
            result = beside(operand)
        return lax.psum(grads, "space"), result, early
    core = lax.axis_index("space") % 2
    half = grads.shape[0] // 2
    pair = [(i, i ^ 1) for i in range(count)]
    across = [(i, i ^ 2) for i in range(count)]
    mine = lax.dynamic_slice_in_dim(grads, core * half, half, axis=0)
    other = lax.dynamic_slice_in_dim(grads, (1 - core) * half, half, axis=0)
    mine = mine + lax.ppermute(other, "space", pair)
    if early is not None:
        mine, early = lax.optimization_barrier((mine, early))
    if beside is not None:
        mine, operand = lax.optimization_barrier((mine, operand))
    arrived = lax.ppermute(mine, "space", across)
    if beside is not None:
        result = beside(operand)
        arrived, result = lax.optimization_barrier((arrived, result))
    mine = mine + arrived
    theirs = lax.ppermute(mine, "space", pair)
    low = jnp.where(core == 0, mine, theirs)
    high = jnp.where(core == 0, theirs, mine)
    return jnp.concatenate([low, high], axis=0), result, early


def chip_slab(rimmed, core):
    depth = rimmed.shape[1] - 2
    pair = [(i, i ^ 1) for i in range(4)]
    send = lax.dynamic_slice_in_dim(rimmed, core * 2, depth, axis=1)
    got = lax.ppermute(send, "space", pair)
    return jnp.where(
        core == 0, jnp.concatenate([rimmed, got], axis=1), jnp.concatenate([got, rimmed], axis=1)
    )


def chip_upstream(upstream, core):
    half = upstream.shape[0] // 2
    pair = [(i, i ^ 1) for i in range(4)]
    mine = lax.dynamic_slice_in_dim(upstream, core * half, half, axis=0)
    send = lax.dynamic_slice_in_dim(upstream, (1 - core) * half, half, axis=0)
    got = lax.ppermute(send, "space", pair)
    return jnp.where(
        core == 0, jnp.concatenate([mine, got], axis=1), jnp.concatenate([got, mine], axis=1)
    )


def chip_sum(mine, core, beside=None, operand=None, early=None):
    pair = [(i, i ^ 1) for i in range(4)]
    across = [(i, i ^ 2) for i in range(4)]
    result = None
    if early is not None:
        mine, early = lax.optimization_barrier((mine, early))
    if beside is not None:
        mine, operand = lax.optimization_barrier((mine, operand))
    arrived = lax.ppermute(mine, "space", across)
    if beside is not None:
        result = beside(operand)
        arrived, result = lax.optimization_barrier((arrived, result))
    mine = mine + arrived
    theirs = lax.ppermute(mine, "space", pair)
    low = jnp.where(core == 0, mine, theirs)
    high = jnp.where(core == 0, theirs, mine)
    return jnp.concatenate([low, high], axis=0), result, early


def on_device(volume, weight, bias, upstream):
    out_dev = weight.shape[0]
    in_all = weight.shape[2]
    in_dev = volume.shape[0]
    depth = upstream.shape[1]
    kernel = weight.reshape(out_dev, 3, 3, 3, in_all).transpose(0, 4, 1, 2, 3)
    paired = lax.axis_size("space") == 4 and out_dev % 2 == 0
    core = lax.axis_index("space") % 2
    if paired:
        chip_up = chip_upstream(upstream, core)
        shifted = plane_shifts(chip_up)
        rows = out_dev // 2
        span = chip_up.shape[1]
    else:
        shifted = plane_shifts(upstream)
    lefts, rights = line_steps(volume, "filt")
    own = padded(volume, (("space", 1),), 1)
    first = min(2, len(lefts))
    tied = lax.optimization_barrier((own, lefts[:first], rights[:first]))
    own, lefts[:first], rights[:first] = tied
    later = (lefts[first:], rights[first:])
    if paired:
        own_part = tap_grads(chip_slab(own, core), shifted, rows, span)
        own_grads, _, later = chip_sum(own_part, core, early=later)
    else:
        own_grads, _, later = space_sum(tap_grads(own, shifted, out_dev, depth), early=later)
    lefts[first:], rights[first:] = later
    rolled = line_gather(volume, "filt", lefts, rights)
    rolled = padded(rolled, (("space", 1),), 1)
    start = lax.axis_index("filt") * in_dev
    rimmed = jnp.roll(rolled, start, axis=0)
    rest = lax.slice_in_dim(rolled, in_dev, in_all, axis=0)

    def forward(slab):
        pre = convolve(slab, kernel) + bias[:, None, None, None]
        return jnp.where(pre > 0, pre, 0.3 * pre).astype(jnp.bfloat16)

    if paired:
        rest_part = tap_grads(chip_slab(rest, core), shifted, rows, span)
        rest_grads, features, own_grads = chip_sum(
            rest_part, core, forward, rimmed, early=own_grads
        )
    else:
        rest_grads, features, own_grads = space_sum(
            tap_grads(rest, shifted, out_dev, depth), forward, rimmed, early=own_grads
        )
    weight_grad = jnp.roll(jnp.concatenate([own_grads, rest_grads], axis=2), start, axis=2)
    return (features, weight_grad)


def solution(mesh):
    return jax.shard_map(
        on_device,
        mesh=mesh,
        in_specs=(
            P("filt", ("parts", "space"), None, None),
            P("filt", None, None),
            P("filt"),
            P("filt", ("parts", "space"), None, None),
        ),
        out_specs=(P("filt", ("parts", "space"), None, None), P(("parts", "filt"), None, None)),
        check_vma=False,
    )
```

```python
import jax
import jax.numpy as jnp
from jax import lax
from jax.sharding import PartitionSpec as P


def padded(block, sides, width):
    for axis, dim in sides:
        count = lax.axis_size(axis)
        forward = [(i, i + 1) for i in range(count - 1)]
        backward = [(target, source) for source, target in forward]
        low = lax.ppermute(
            lax.slice_in_dim(block, block.shape[dim] - width, None, axis=dim), axis, forward
        )
        high = lax.ppermute(lax.slice_in_dim(block, 0, width, axis=dim), axis, backward)
        block = jnp.concatenate([low, block, high], axis=dim)
    return block


def convolve(slab, kernel):
    return lax.conv_general_dilated(
        slab[None],
        kernel,
        (1, 1, 1),
        [(0, 0), (1, 1), (1, 1)],
        dimension_numbers=("NCDHW", "OIDHW", "NCDHW"),
        preferred_element_type=jnp.float32,
    )[0]


def plane_shifts(upstream):
    height = upstream.shape[2]
    length = upstream.shape[3]
    spread = jnp.pad(upstream, ((0, 0), (0, 0), (1, 1), (1, 1)))
    copies = []
    for tap in range(9):
        second = tap // 3
        third = tap % 3
        copies.append(
            spread[:, :, 2 - second : 2 - second + height, 2 - third : 2 - third + length]
        )
    stacked = jnp.stack(copies, 1)
    return stacked.reshape(upstream.shape[0] * 9, -1)


def tap_grads(rimmed, shifted, out_dev, depth):
    split = 2 if out_dev % 2 == 0 else 1
    rows = []
    for first in range(3):
        window = lax.slice_in_dim(rimmed, first, first + depth, axis=1)
        flat = window.reshape(window.shape[0], -1)
        product = lax.dot_general(
            shifted, flat, (((1,), (1,)), ((), ())), preferred_element_type=jnp.float32
        )
        rows.append(product.reshape(split, out_dev // split, 9, window.shape[0]))
    return jnp.concatenate(rows, axis=2)


def line_steps(block, axis):
    count = lax.axis_size(axis)
    lefts, rights = [], []
    from_left = block
    from_right = block
    for step in range(1, count):
        from_left = lax.ppermute(
            from_left, axis, [(i, i + 1) for i in range(step - 1, count - 1)]
        )
        from_right = lax.ppermute(
            from_right, axis, [(i, i - 1) for i in range(1, count - step + 1)]
        )
        lefts.append(from_left)
        rights.append(from_right)
    return lefts, rights


def line_gather(block, axis, lefts, rights):
    count = lax.axis_size(axis)
    here = lax.axis_index(axis)
    blocks = [block]
    for k in range(1, count):
        blocks.append(jnp.where(here + k < count, rights[k - 1], lefts[count - k - 1]))
    return jnp.concatenate(blocks, axis=0)


def space_sum(grads, beside=None, operand=None, early=None):
    count = lax.axis_size("space")
    result = None
    if count != 4 or grads.shape[0] != 2:
        if beside is not None:
            result = beside(operand)
        flat = grads.reshape((-1,) + grads.shape[2:])
        return lax.psum(flat, "space"), result, early
    core = lax.axis_index("space") % 2
    pair = [(i, i ^ 1) for i in range(count)]
    across = [(i, i ^ 2) for i in range(count)]
    mine = lax.dynamic_index_in_dim(grads, core, axis=0, keepdims=False)
    other = lax.dynamic_index_in_dim(grads, 1 - core, axis=0, keepdims=False)
    mine = mine + lax.ppermute(other, "space", pair)
    if early is not None:
        mine, early = lax.optimization_barrier((mine, early))
    if beside is not None:
        mine, operand = lax.optimization_barrier((mine, operand))
    arrived = lax.ppermute(mine, "space", across)
    if beside is not None:
        result = beside(operand)
        arrived, result = lax.optimization_barrier((arrived, result))
    mine = mine + arrived
    theirs = lax.ppermute(mine, "space", pair)
    low = jnp.where(core == 0, mine, theirs)
    high = jnp.where(core == 0, theirs, mine)
    return jnp.concatenate([low, high], axis=0), result, early


def on_device(volume, weight, bias, upstream):
    out_dev = weight.shape[0]
    in_all = weight.shape[2]
    in_dev = volume.shape[0]
    depth = upstream.shape[1]
    kernel = weight.reshape(out_dev, 3, 3, 3, in_all).transpose(0, 4, 1, 2, 3)
    shifted = plane_shifts(upstream)
    lefts, rights = line_steps(volume, "filt")
    own = padded(volume, (("space", 1),), 1)
    first = min(2, len(lefts))
    tied = lax.optimization_barrier((own, lefts[:first], rights[:first]))
    own, lefts[:first], rights[:first] = tied
    later = (lefts[first:], rights[first:])
    own_grads, _, later = space_sum(tap_grads(own, shifted, out_dev, depth), early=later)
    lefts[first:], rights[first:] = later
    rolled = line_gather(volume, "filt", lefts, rights)
    rolled = padded(rolled, (("space", 1),), 1)
    start = lax.axis_index("filt") * in_dev
    rimmed = jnp.roll(rolled, start, axis=0)
    rest = lax.slice_in_dim(rolled, in_dev, in_all, axis=0)

    def forward(slab):
        pre = convolve(slab, kernel) + bias[:, None, None, None]
        return jnp.where(pre > 0, pre, 0.3 * pre).astype(jnp.bfloat16)

    rest_grads, features, own_grads = space_sum(
        tap_grads(rest, shifted, out_dev, depth), forward, rimmed, early=own_grads
    )
    weight_grad = jnp.roll(jnp.concatenate([own_grads, rest_grads], axis=2), start, axis=2)
    return (features, weight_grad)


def solution(mesh):
    return jax.shard_map(
        on_device,
        mesh=mesh,
        in_specs=(
            P("filt", ("parts", "space"), None, None),
            P("filt", None, None),
            P("filt"),
            P("filt", ("parts", "space"), None, None),
        ),
        out_specs=(P("filt", ("parts", "space"), None, None), P(("parts", "filt"), None, None)),
        check_vma=False,
    )
```

```python
import jax
import jax.numpy as jnp
from jax import lax
from jax.sharding import PartitionSpec as P


def padded(block, sides, width):
    for axis, dim in sides:
        count = lax.axis_size(axis)
        forward = [(i, i + 1) for i in range(count - 1)]
        backward = [(target, source) for source, target in forward]
        low = lax.ppermute(
            lax.slice_in_dim(block, block.shape[dim] - width, None, axis=dim), axis, forward
        )
        high = lax.ppermute(lax.slice_in_dim(block, 0, width, axis=dim), axis, backward)
        block = jnp.concatenate([low, block, high], axis=dim)
    return block


def convolve(slab, kernel):
    return lax.conv_general_dilated(
        slab[None],
        kernel,
        (1, 1, 1),
        [(0, 0), (1, 1), (1, 1)],
        dimension_numbers=("NCDHW", "OIDHW", "NCDHW"),
        preferred_element_type=jnp.float32,
    )[0]


def plane_shifts(upstream):
    height = upstream.shape[2]
    length = upstream.shape[3]
    spread = jnp.pad(upstream, ((0, 0), (0, 0), (1, 1), (1, 1)))
    copies = []
    for tap in range(9):
        second = tap // 3
        third = tap % 3
        copies.append(
            spread[:, :, 2 - second : 2 - second + height, 2 - third : 2 - third + length]
        )
    stacked = jnp.stack(copies, 1)
    return stacked.reshape(upstream.shape[0] * 9, -1)


def tap_grads(rimmed, shifted, out_dev, depth):
    rows = []
    for first in range(3):
        window = lax.slice_in_dim(rimmed, first, first + depth, axis=1)
        flat = window.reshape(window.shape[0], -1)
        product = lax.dot_general(
            shifted, flat, (((1,), (1,)), ((), ())), preferred_element_type=jnp.float32
        )
        rows.append(product.reshape(out_dev, 9, window.shape[0]))
    return jnp.concatenate(rows, axis=1)


def line_steps(block, axis):
    count = lax.axis_size(axis)
    lefts, rights = [], []
    from_left = block
    from_right = block
    for step in range(1, count):
        from_left = lax.ppermute(
            from_left, axis, [(i, i + 1) for i in range(step - 1, count - 1)]
        )
        from_right = lax.ppermute(
            from_right, axis, [(i, i - 1) for i in range(1, count - step + 1)]
        )
        lefts.append(from_left)
        rights.append(from_right)
    return lefts, rights


def line_gather(block, axis, lefts, rights):
    count = lax.axis_size(axis)
    here = lax.axis_index(axis)
    blocks = [block]
    for k in range(1, count):
        blocks.append(jnp.where(here + k < count, rights[k - 1], lefts[count - k - 1]))
    return jnp.concatenate(blocks, axis=0)


def space_sum(grads, beside=None, operand=None, early=None):
    count = lax.axis_size("space")
    result = None
    if count != 4 or grads.shape[0] % 2:
        if beside is not None:
            result = beside(operand)
        return lax.psum(grads, "space"), result, early
    core = lax.axis_index("space") % 2
    half = grads.shape[0] // 2
    pair = [(i, i ^ 1) for i in range(count)]
    across = [(i, i ^ 2) for i in range(count)]
    mine = lax.dynamic_slice_in_dim(grads, core * half, half, axis=0)
    other = lax.dynamic_slice_in_dim(grads, (1 - core) * half, half, axis=0)
    mine = mine + lax.ppermute(other, "space", pair)
    if early is not None:
        mine, early = lax.optimization_barrier((mine, early))
    if beside is not None:
        mine, operand = lax.optimization_barrier((mine, operand))
    arrived = lax.ppermute(mine, "space", across)
    if beside is not None:
        result = beside(operand)
        arrived, result = lax.optimization_barrier((arrived, result))
    mine = mine + arrived
    theirs = lax.ppermute(mine, "space", pair)
    low = jnp.where(core == 0, mine, theirs)
    high = jnp.where(core == 0, theirs, mine)
    return jnp.concatenate([low, high], axis=0), result, early


def on_device(volume, weight, bias, upstream):
    out_dev = weight.shape[0]
    in_all = weight.shape[2]
    in_dev = volume.shape[0]
    depth = upstream.shape[1]
    kernel = weight.reshape(out_dev, 3, 3, 3, in_all).transpose(0, 4, 1, 2, 3)
    shifted = plane_shifts(upstream)
    lefts, rights = line_steps(volume, "filt")
    own = padded(volume, (("space", 1),), 1)
    first = min(2, len(lefts))
    tied = lax.optimization_barrier((own, lefts[:first], rights[:first]))
    own, lefts[:first], rights[:first] = tied
    later = (lefts[first:], rights[first:])
    own_part, later = lax.optimization_barrier((tap_grads(own, shifted, out_dev, depth), later))
    own_grads = lax.psum(own_part, "space")
    lefts[first:], rights[first:] = later
    rolled = line_gather(volume, "filt", lefts, rights)
    rolled = padded(rolled, (("space", 1),), 1)
    start = lax.axis_index("filt") * in_dev
    rimmed = jnp.roll(rolled, start, axis=0)
    rest = lax.slice_in_dim(rolled, in_dev, in_all, axis=0)

    def forward(slab):
        pre = convolve(slab, kernel) + bias[:, None, None, None]
        return jnp.where(pre > 0, pre, 0.3 * pre).astype(jnp.bfloat16)

    rest_grads, features, own_grads = space_sum(
        tap_grads(rest, shifted, out_dev, depth), forward, rimmed, early=own_grads
    )
    weight_grad = jnp.roll(jnp.concatenate([own_grads, rest_grads], axis=2), start, axis=2)
    return (features, weight_grad)


def solution(mesh):
    return jax.shard_map(
        on_device,
        mesh=mesh,
        in_specs=(
            P("filt", ("parts", "space"), None, None),
            P("filt", None, None),
            P("filt"),
            P("filt", ("parts", "space"), None, None),
        ),
        out_specs=(P("filt", ("parts", "space"), None, None), P(("parts", "filt"), None, None)),
        check_vma=False,
    )
```

```python
import jax
import jax.numpy as jnp
from jax import lax
from jax.sharding import PartitionSpec as P


def padded(block, sides, width):
    for axis, dim in sides:
        count = lax.axis_size(axis)
        forward = [(i, i + 1) for i in range(count - 1)]
        backward = [(target, source) for source, target in forward]
        low = lax.ppermute(
            lax.slice_in_dim(block, block.shape[dim] - width, None, axis=dim), axis, forward
        )
        high = lax.ppermute(lax.slice_in_dim(block, 0, width, axis=dim), axis, backward)
        block = jnp.concatenate([low, block, high], axis=dim)
    return block


def convolve(slab, kernel):
    return lax.conv_general_dilated(
        slab[None],
        kernel,
        (1, 1, 1),
        [(0, 0), (1, 1), (1, 1)],
        dimension_numbers=("NCDHW", "OIDHW", "NCDHW"),
        preferred_element_type=jnp.float32,
    )[0]


def plane_shifts(upstream):
    height = upstream.shape[2]
    length = upstream.shape[3]
    spread = jnp.pad(upstream, ((0, 0), (0, 0), (1, 1), (1, 1)))
    copies = []
    for tap in range(9):
        second = tap // 3
        third = tap % 3
        copies.append(
            spread[:, :, 2 - second : 2 - second + height, 2 - third : 2 - third + length]
        )
    stacked = jnp.stack(copies, 1)
    return stacked.reshape(upstream.shape[0] * 9, -1)


def tap_grads(rimmed, shifted, out_dev, depth):
    rows = []
    for first in range(3):
        window = lax.slice_in_dim(rimmed, first, first + depth, axis=1)
        flat = window.reshape(window.shape[0], -1)
        product = lax.dot_general(
            shifted, flat, (((1,), (1,)), ((), ())), preferred_element_type=jnp.float32
        )
        rows.append(product.reshape(out_dev, 9, window.shape[0]))
    return jnp.concatenate(rows, axis=1)


def line_steps(block, axis):
    count = lax.axis_size(axis)
    lefts, rights = [], []
    from_left = block
    from_right = block
    for step in range(1, count):
        from_left = lax.ppermute(
            from_left, axis, [(i, i + 1) for i in range(step - 1, count - 1)]
        )
        from_right = lax.ppermute(
            from_right, axis, [(i, i - 1) for i in range(1, count - step + 1)]
        )
        lefts.append(from_left)
        rights.append(from_right)
    return lefts, rights


def line_gather(block, axis, lefts, rights):
    count = lax.axis_size(axis)
    here = lax.axis_index(axis)
    blocks = [block]
    for k in range(1, count):
        blocks.append(jnp.where(here + k < count, rights[k - 1], lefts[count - k - 1]))
    return jnp.concatenate(blocks, axis=0)


def space_sum(grads, beside=None, operand=None, early=None):
    count = lax.axis_size("space")
    result = None
    if count != 4 or grads.shape[0] % 2:
        if beside is not None:
            result = beside(operand)
        return lax.psum(grads, "space"), result, early
    core = lax.axis_index("space") % 2
    half = grads.shape[0] // 2
    pair = [(i, i ^ 1) for i in range(count)]
    across = [(i, i ^ 2) for i in range(count)]
    mine = lax.dynamic_slice_in_dim(grads, core * half, half, axis=0)
    other = lax.dynamic_slice_in_dim(grads, (1 - core) * half, half, axis=0)
    mine = mine + lax.ppermute(other, "space", pair)
    if early is not None:
        mine, early = lax.optimization_barrier((mine, early))
    if beside is not None:
        mine, operand = lax.optimization_barrier((mine, operand))
    arrived = lax.ppermute(mine, "space", across)
    if beside is not None:
        result = beside(operand)
        arrived, result = lax.optimization_barrier((arrived, result))
    mine = mine + arrived
    theirs = lax.ppermute(mine, "space", pair)
    low = jnp.where(core == 0, mine, theirs)
    high = jnp.where(core == 0, theirs, mine)
    return jnp.concatenate([low, high], axis=0), result, early


def on_device(volume, weight, bias, upstream):
    out_dev = weight.shape[0]
    in_all = weight.shape[2]
    in_dev = volume.shape[0]
    depth = upstream.shape[1]
    kernel = weight.reshape(out_dev, 3, 3, 3, in_all).transpose(0, 4, 1, 2, 3)
    shifted = plane_shifts(upstream)
    lefts, rights = line_steps(volume, "filt")
    own = padded(volume, (("space", 1),), 1)
    first = min(2, len(lefts))
    tied = lax.optimization_barrier((own, lefts[:first], rights[:first]))
    own, lefts[:first], rights[:first] = tied
    later = (lefts[first:], rights[first:])
    own_part = tap_grads(own, shifted, out_dev, depth)
    if lax.axis_size("space") == 4 and out_dev % 2 == 0:
        core = lax.axis_index("space") % 2
        half = out_dev // 2
        pair = [(i, i ^ 1) for i in range(4)]
        across = [(i, i ^ 2) for i in range(4)]
        mine = lax.dynamic_slice_in_dim(own_part, core * half, half, axis=0)
        other = lax.dynamic_slice_in_dim(own_part, (1 - core) * half, half, axis=0)
        mine = mine + lax.ppermute(other, "space", pair)
        mine, later = lax.optimization_barrier((mine, later))
        lefts[first:], rights[first:] = later
        rolled = line_gather(volume, "filt", lefts, rights)
        rolled = padded(rolled, (("space", 1),), 1)
        mine, rolled = lax.optimization_barrier((mine, rolled))
        mine = mine + lax.ppermute(mine, "space", across)
        theirs = lax.ppermute(mine, "space", pair)
        low = jnp.where(core == 0, mine, theirs)
        high = jnp.where(core == 0, theirs, mine)
        own_grads = jnp.concatenate([low, high], axis=0)
    else:
        own_grads, _, later = space_sum(own_part, early=later)
        lefts[first:], rights[first:] = later
        rolled = line_gather(volume, "filt", lefts, rights)
        rolled = padded(rolled, (("space", 1),), 1)
    start = lax.axis_index("filt") * in_dev
    rimmed = jnp.roll(rolled, start, axis=0)
    rest = lax.slice_in_dim(rolled, in_dev, in_all, axis=0)

    def forward(slab):
        pre = convolve(slab, kernel) + bias[:, None, None, None]
        return jnp.where(pre > 0, pre, 0.3 * pre).astype(jnp.bfloat16)

    rest_grads, features, own_grads = space_sum(
        tap_grads(rest, shifted, out_dev, depth), forward, rimmed, early=own_grads
    )
    weight_grad = jnp.roll(jnp.concatenate([own_grads, rest_grads], axis=2), start, axis=2)
    return (features, weight_grad)


def solution(mesh):
    return jax.shard_map(
        on_device,
        mesh=mesh,
        in_specs=(
            P("filt", ("parts", "space"), None, None),
            P("filt", None, None),
            P("filt"),
            P("filt", ("parts", "space"), None, None),
        ),
        out_specs=(P("filt", ("parts", "space"), None, None), P(("parts", "filt"), None, None)),
        check_vma=False,
    )
```

```python
import jax
import jax.numpy as jnp
from jax import lax
from jax.sharding import PartitionSpec as P


def padded(block, sides, width):
    for axis, dim in sides:
        count = lax.axis_size(axis)
        forward = [(i, i + 1) for i in range(count - 1)]
        backward = [(target, source) for source, target in forward]
        low = lax.ppermute(
            lax.slice_in_dim(block, block.shape[dim] - width, None, axis=dim), axis, forward
        )
        high = lax.ppermute(lax.slice_in_dim(block, 0, width, axis=dim), axis, backward)
        block = jnp.concatenate([low, block, high], axis=dim)
    return block


def rims(block, axis):
    count = lax.axis_size(axis)
    forward = [(i, i + 1) for i in range(count - 1)]
    backward = [(target, source) for source, target in forward]
    low = lax.ppermute(lax.slice_in_dim(block, block.shape[1] - 1, None, axis=1), axis, forward)
    high = lax.ppermute(lax.slice_in_dim(block, 0, 1, axis=1), axis, backward)
    return low, high


def side_grads(block, low, high, shifted, out_dev):
    depth = block.shape[1]
    windows = [
        jnp.concatenate([low, lax.slice_in_dim(block, 0, depth - 1, axis=1)], axis=1),
        block,
        jnp.concatenate([lax.slice_in_dim(block, 1, depth, axis=1), high], axis=1),
    ]
    rows = [None, None, None]
    for first in (1, 0, 2):
        flat = windows[first].reshape(block.shape[0], -1)
        product = lax.dot_general(
            shifted, flat, (((1,), (1,)), ((), ())), preferred_element_type=jnp.float32
        )
        rows[first] = product.reshape(out_dev, 9, block.shape[0])
    return jnp.concatenate(rows, axis=1)


def convolve(slab, kernel):
    return lax.conv_general_dilated(
        slab[None],
        kernel,
        (1, 1, 1),
        [(0, 0), (1, 1), (1, 1)],
        dimension_numbers=("NCDHW", "OIDHW", "NCDHW"),
        preferred_element_type=jnp.float32,
    )[0]


def plane_shifts(upstream):
    height = upstream.shape[2]
    length = upstream.shape[3]
    spread = jnp.pad(upstream, ((0, 0), (0, 0), (1, 1), (1, 1)))
    copies = []
    for tap in range(9):
        second = tap // 3
        third = tap % 3
        copies.append(
            spread[:, :, 2 - second : 2 - second + height, 2 - third : 2 - third + length]
        )
    stacked = jnp.stack(copies, 1)
    return stacked.reshape(upstream.shape[0] * 9, -1)


def tap_grads(rimmed, shifted, out_dev, depth):
    rows = []
    for first in range(3):
        window = lax.slice_in_dim(rimmed, first, first + depth, axis=1)
        flat = window.reshape(window.shape[0], -1)
        product = lax.dot_general(
            shifted, flat, (((1,), (1,)), ((), ())), preferred_element_type=jnp.float32
        )
        rows.append(product.reshape(out_dev, 9, window.shape[0]))
    return jnp.concatenate(rows, axis=1)


def line_steps(block, axis):
    count = lax.axis_size(axis)
    lefts, rights = [], []
    from_left = block
    from_right = block
    for step in range(1, count):
        from_left = lax.ppermute(
            from_left, axis, [(i, i + 1) for i in range(step - 1, count - 1)]
        )
        from_right = lax.ppermute(
            from_right, axis, [(i, i - 1) for i in range(1, count - step + 1)]
        )
        lefts.append(from_left)
        rights.append(from_right)
    return lefts, rights


def line_gather(block, axis, lefts, rights):
    count = lax.axis_size(axis)
    here = lax.axis_index(axis)
    blocks = [block]
    for k in range(1, count):
        blocks.append(jnp.where(here + k < count, rights[k - 1], lefts[count - k - 1]))
    return jnp.concatenate(blocks, axis=0)


def space_sum(grads, beside=None, operand=None, early=None):
    count = lax.axis_size("space")
    result = None
    if count != 4 or grads.shape[0] % 2:
        if beside is not None:
            result = beside(operand)
        return lax.psum(grads, "space"), result, early
    core = lax.axis_index("space") % 2
    half = grads.shape[0] // 2
    pair = [(i, i ^ 1) for i in range(count)]
    across = [(i, i ^ 2) for i in range(count)]
    mine = lax.dynamic_slice_in_dim(grads, core * half, half, axis=0)
    other = lax.dynamic_slice_in_dim(grads, (1 - core) * half, half, axis=0)
    mine = mine + lax.ppermute(other, "space", pair)
    if early is not None:
        mine, early = lax.optimization_barrier((mine, early))
    if beside is not None:
        mine, operand = lax.optimization_barrier((mine, operand))
    arrived = lax.ppermute(mine, "space", across)
    if beside is not None:
        result = beside(operand)
        arrived, result = lax.optimization_barrier((arrived, result))
    mine = mine + arrived
    theirs = lax.ppermute(mine, "space", pair)
    low = jnp.where(core == 0, mine, theirs)
    high = jnp.where(core == 0, theirs, mine)
    return jnp.concatenate([low, high], axis=0), result, early


def on_device(volume, weight, bias, upstream):
    out_dev = weight.shape[0]
    in_all = weight.shape[2]
    in_dev = volume.shape[0]
    depth = upstream.shape[1]
    kernel = weight.reshape(out_dev, 3, 3, 3, in_all).transpose(0, 4, 1, 2, 3)
    shifted = plane_shifts(upstream)
    lefts, rights = line_steps(volume, "filt")
    own = padded(volume, (("space", 1),), 1)
    first = min(2, len(lefts))
    tied = lax.optimization_barrier((own, lefts[:first], rights[:first]))
    own, lefts[:first], rights[:first] = tied
    later = (lefts[first:], rights[first:])
    own_grads, _, later = space_sum(tap_grads(own, shifted, out_dev, depth), early=later)
    lefts[first:], rights[first:] = later
    rolled = line_gather(volume, "filt", lefts, rights)
    low, high = rims(rolled, "space")
    start = lax.axis_index("filt") * in_dev
    rimmed = jnp.roll(jnp.concatenate([low, rolled, high], axis=1), start, axis=0)
    rest_part = side_grads(
        lax.slice_in_dim(rolled, in_dev, in_all, axis=0),
        lax.slice_in_dim(low, in_dev, in_all, axis=0),
        lax.slice_in_dim(high, in_dev, in_all, axis=0),
        shifted,
        out_dev,
    )

    def forward(slab):
        pre = convolve(slab, kernel) + bias[:, None, None, None]
        return jnp.where(pre > 0, pre, 0.3 * pre).astype(jnp.bfloat16)

    rest_grads, features, own_grads = space_sum(
        rest_part, forward, rimmed, early=own_grads
    )
    weight_grad = jnp.roll(jnp.concatenate([own_grads, rest_grads], axis=2), start, axis=2)
    return (features, weight_grad)


def solution(mesh):
    return jax.shard_map(
        on_device,
        mesh=mesh,
        in_specs=(
            P("filt", ("parts", "space"), None, None),
            P("filt", None, None),
            P("filt"),
            P("filt", ("parts", "space"), None, None),
        ),
        out_specs=(P("filt", ("parts", "space"), None, None), P(("parts", "filt"), None, None)),
        check_vma=False,
    )
```

```python
import jax
import jax.numpy as jnp
from jax import lax
from jax.sharding import PartitionSpec as P


def padded(block, sides, width):
    for axis, dim in sides:
        count = lax.axis_size(axis)
        forward = [(i, i + 1) for i in range(count - 1)]
        backward = [(target, source) for source, target in forward]
        low = lax.ppermute(
            lax.slice_in_dim(block, block.shape[dim] - width, None, axis=dim), axis, forward
        )
        high = lax.ppermute(lax.slice_in_dim(block, 0, width, axis=dim), axis, backward)
        block = jnp.concatenate([low, block, high], axis=dim)
    return block


def convolve(slab, kernel):
    return lax.conv_general_dilated(
        slab[None],
        kernel,
        (1, 1, 1),
        [(0, 0), (1, 1), (1, 1)],
        dimension_numbers=("NCDHW", "OIDHW", "NCDHW"),
        preferred_element_type=jnp.float32,
    )[0]


def plane_shifts(upstream):
    height = upstream.shape[2]
    length = upstream.shape[3]
    spread = jnp.pad(upstream, ((0, 0), (0, 0), (1, 1), (1, 1)))
    copies = []
    for tap in range(9):
        second = tap // 3
        third = tap % 3
        copies.append(
            spread[:, :, 2 - second : 2 - second + height, 2 - third : 2 - third + length]
        )
    stacked = jnp.stack(copies, 1)
    return stacked.reshape(upstream.shape[0] * 9, -1)


def tap_grads(rimmed, shifted, out_dev, depth):
    rows = []
    for first in range(3):
        window = lax.slice_in_dim(rimmed, first, first + depth, axis=1)
        flat = window.reshape(window.shape[0], -1)
        product = lax.dot_general(
            shifted, flat, (((1,), (1,)), ((), ())), preferred_element_type=jnp.float32
        )
        rows.append(product.reshape(out_dev, 9, window.shape[0]))
    return jnp.concatenate(rows, axis=1)


def line_steps(block, axis):
    count = lax.axis_size(axis)
    lefts, rights = [], []
    from_left = block
    from_right = block
    for step in range(1, count):
        from_left = lax.ppermute(
            from_left, axis, [(i, i + 1) for i in range(step - 1, count - 1)]
        )
        from_right = lax.ppermute(
            from_right, axis, [(i, i - 1) for i in range(1, count - step + 1)]
        )
        lefts.append(from_left)
        rights.append(from_right)
    return lefts, rights


def line_gather(block, axis, lefts, rights):
    count = lax.axis_size(axis)
    here = lax.axis_index(axis)
    blocks = [block]
    for k in range(1, count):
        blocks.append(jnp.where(here + k < count, rights[k - 1], lefts[count - k - 1]))
    return jnp.concatenate(blocks, axis=0)


def space_sum(grads, beside=None, operand=None, early=None):
    count = lax.axis_size("space")
    result = None
    if count != 4 or grads.shape[0] % 2:
        if beside is not None:
            result = beside(operand)
        return lax.psum(grads, "space"), result, early
    core = lax.axis_index("space") % 2
    half = grads.shape[0] // 2
    pair = [(i, i ^ 1) for i in range(count)]
    across = [(i, i ^ 2) for i in range(count)]
    mine = lax.dynamic_slice_in_dim(grads, core * half, half, axis=0)
    other = lax.dynamic_slice_in_dim(grads, (1 - core) * half, half, axis=0)
    mine = mine + lax.ppermute(other, "space", pair)
    if early is not None:
        mine, early = lax.optimization_barrier((mine, early))
    if beside is not None:
        mine, operand = lax.optimization_barrier((mine, operand))
    arrived = lax.ppermute(mine, "space", across)
    if beside is not None:
        result = beside(operand)
        arrived, result = lax.optimization_barrier((arrived, result))
    mine = mine + arrived
    theirs = lax.ppermute(mine, "space", pair)
    low = jnp.where(core == 0, mine, theirs)
    high = jnp.where(core == 0, theirs, mine)
    return jnp.concatenate([low, high], axis=0), result, early


def on_device(volume, weight, bias, upstream):
    out_dev = weight.shape[0]
    in_all = weight.shape[2]
    in_dev = volume.shape[0]
    depth = upstream.shape[1]
    kernel = weight.reshape(out_dev, 3, 3, 3, in_all).transpose(0, 4, 1, 2, 3)
    shifted = plane_shifts(upstream)
    lefts, rights = line_steps(volume, "filt")
    own = padded(volume, (("space", 1),), 1)
    first = min(2, len(lefts))
    tied = lax.optimization_barrier((own, lefts[:first], rights[:first]))
    own, lefts[:first], rights[:first] = tied
    later = (lefts[first:], rights[first:])
    own_grads, _, later = space_sum(tap_grads(own, shifted, out_dev, depth), early=later)
    lefts[first:], rights[first:] = later
    rolled = line_gather(volume, "filt", lefts, rights)
    rolled = padded(rolled, (("space", 1),), 1)
    start = lax.axis_index("filt") * in_dev
    rimmed = jnp.roll(rolled, start, axis=0)
    rest = lax.slice_in_dim(rolled, in_dev, in_all, axis=0)

    def forward(slab):
        pre = convolve(slab, kernel) + bias[:, None, None, None]
        return jnp.where(pre > 0, pre, 0.3 * pre).astype(jnp.bfloat16)

    rest_grads, features, own_grads = space_sum(
        tap_grads(rest, shifted, out_dev, depth), forward, rimmed, early=own_grads
    )
    ordered = jnp.concatenate([own_grads, rest_grads], axis=2)
    blocks = in_all // in_dev
    here = lax.axis_index("filt")
    pieces = [
        lax.dynamic_slice_in_dim(ordered, ((g - here) % blocks) * in_dev, in_dev, axis=2)
        for g in range(blocks)
    ]
    weight_grad = jnp.concatenate(pieces, axis=2)
    return (features, weight_grad)


def solution(mesh):
    return jax.shard_map(
        on_device,
        mesh=mesh,
        in_specs=(
            P("filt", ("parts", "space"), None, None),
            P("filt", None, None),
            P("filt"),
            P("filt", ("parts", "space"), None, None),
        ),
        out_specs=(P("filt", ("parts", "space"), None, None), P(("parts", "filt"), None, None)),
        check_vma=False,
    )
```

```python
import jax
import jax.numpy as jnp
from jax import lax
from jax.sharding import PartitionSpec as P


def padded(block, sides, width):
    for axis, dim in sides:
        count = lax.axis_size(axis)
        forward = [(i, i + 1) for i in range(count - 1)]
        backward = [(target, source) for source, target in forward]
        low = lax.ppermute(
            lax.slice_in_dim(block, block.shape[dim] - width, None, axis=dim), axis, forward
        )
        high = lax.ppermute(lax.slice_in_dim(block, 0, width, axis=dim), axis, backward)
        block = jnp.concatenate([low, block, high], axis=dim)
    return block


def convolve(slab, kernel):
    return lax.conv_general_dilated(
        slab[None],
        kernel,
        (1, 1, 1),
        [(0, 0), (1, 1), (1, 1)],
        dimension_numbers=("NCDHW", "OIDHW", "NCDHW"),
        preferred_element_type=jnp.float32,
    )[0]


def plane_shifts(upstream):
    height = upstream.shape[2]
    length = upstream.shape[3]
    spread = jnp.pad(upstream, ((0, 0), (0, 0), (1, 1), (1, 1)))
    copies = []
    for tap in range(9):
        second = tap // 3
        third = tap % 3
        copies.append(
            spread[:, :, 2 - second : 2 - second + height, 2 - third : 2 - third + length]
        )
    stacked = jnp.stack(copies, 1)
    return stacked.reshape(upstream.shape[0] * 9, -1)


def tap_grads(rimmed, shifted, out_dev, depth):
    rows = []
    for first in range(3):
        window = lax.slice_in_dim(rimmed, first, first + depth, axis=1)
        flat = window.reshape(window.shape[0], -1)
        product = lax.dot_general(
            shifted, flat, (((1,), (1,)), ((), ())), preferred_element_type=jnp.float32
        )
        rows.append(product.reshape(out_dev, 9, window.shape[0]))
    return jnp.concatenate(rows, axis=1)


def line_steps(block, axis):
    count = lax.axis_size(axis)
    lefts, rights = [], []
    from_left = block
    from_right = block
    for step in range(1, count):
        from_left = lax.ppermute(
            from_left, axis, [(i, i + 1) for i in range(step - 1, count - 1)]
        )
        from_right = lax.ppermute(
            from_right, axis, [(i, i - 1) for i in range(1, count - step + 1)]
        )
        lefts.append(from_left)
        rights.append(from_right)
    return lefts, rights


def line_gather(block, axis, lefts, rights):
    count = lax.axis_size(axis)
    here = lax.axis_index(axis)
    blocks = [block]
    for k in range(1, count):
        blocks.append(jnp.where(here + k < count, rights[k - 1], lefts[count - k - 1]))
    return jnp.concatenate(blocks, axis=0)


def space_sum(grads, beside=None, operand=None, early=None):
    count = lax.axis_size("space")
    result = None
    if count != 4 or grads.shape[0] % 2:
        if beside is not None:
            result = beside(operand)
        return lax.psum(grads, "space"), result, early
    core = lax.axis_index("space") % 2
    half = grads.shape[0] // 2
    pair = [(i, i ^ 1) for i in range(count)]
    across = [(i, i ^ 2) for i in range(count)]
    mine = lax.dynamic_slice_in_dim(grads, core * half, half, axis=0)
    other = lax.dynamic_slice_in_dim(grads, (1 - core) * half, half, axis=0)
    mine = mine + lax.ppermute(other, "space", pair)
    if early is not None:
        mine, early = lax.optimization_barrier((mine, early))
    if beside is not None:
        mine, operand = lax.optimization_barrier((mine, operand))
    arrived = lax.ppermute(mine, "space", across)
    if beside is not None:
        result = beside(operand)
        arrived, result = lax.optimization_barrier((arrived, result))
    mine = mine + arrived
    theirs = lax.ppermute(mine, "space", pair)
    low = jnp.where(core == 0, mine, theirs)
    high = jnp.where(core == 0, theirs, mine)
    return jnp.concatenate([low, high], axis=0), result, early


def on_device(volume, weight, bias, upstream):
    out_dev = weight.shape[0]
    in_all = weight.shape[2]
    in_dev = volume.shape[0]
    depth = upstream.shape[1]
    kernel = weight.reshape(out_dev, 3, 3, 3, in_all).transpose(0, 4, 1, 2, 3)
    shifted = plane_shifts(upstream)
    lefts, rights = line_steps(volume, "filt")
    own = padded(volume, (("space", 1),), 1)
    first = min(2, len(lefts))
    tied = lax.optimization_barrier((own, lefts[:first], rights[:first]))
    own, lefts[:first], rights[:first] = tied
    own_grads, _, _ = space_sum(tap_grads(own, shifted, out_dev, depth))
    rolled = line_gather(volume, "filt", lefts, rights)
    rolled = padded(rolled, (("space", 1),), 1)
    start = lax.axis_index("filt") * in_dev
    rimmed = jnp.roll(rolled, start, axis=0)
    rest = lax.slice_in_dim(rolled, in_dev, in_all, axis=0)

    def forward(slab):
        pre = convolve(slab, kernel) + bias[:, None, None, None]
        return jnp.where(pre > 0, pre, 0.3 * pre).astype(jnp.bfloat16)

    rest_grads, features, own_grads = space_sum(
        tap_grads(rest, shifted, out_dev, depth), forward, rimmed, early=own_grads
    )
    ordered = jnp.concatenate([own_grads, rest_grads], axis=2)
    blocks = in_all // in_dev
    here = lax.axis_index("filt")
    pieces = [
        lax.dynamic_slice_in_dim(ordered, ((g - here) % blocks) * in_dev, in_dev, axis=2)
        for g in range(blocks)
    ]
    weight_grad = jnp.concatenate(pieces, axis=2)
    return (features, weight_grad)


def solution(mesh):
    return jax.shard_map(
        on_device,
        mesh=mesh,
        in_specs=(
            P("filt", ("parts", "space"), None, None),
            P("filt", None, None),
            P("filt"),
            P("filt", ("parts", "space"), None, None),
        ),
        out_specs=(P("filt", ("parts", "space"), None, None), P(("parts", "filt"), None, None)),
        check_vma=False,
    )
```

```python
import jax
import jax.numpy as jnp
from jax import lax
from jax.sharding import PartitionSpec as P


def padded(block, sides, width):
    for axis, dim in sides:
        count = lax.axis_size(axis)
        forward = [(i, i + 1) for i in range(count - 1)]
        backward = [(target, source) for source, target in forward]
        low = lax.ppermute(
            lax.slice_in_dim(block, block.shape[dim] - width, None, axis=dim), axis, forward
        )
        high = lax.ppermute(lax.slice_in_dim(block, 0, width, axis=dim), axis, backward)
        block = jnp.concatenate([low, block, high], axis=dim)
    return block


def convolve(slab, kernel):
    return lax.conv_general_dilated(
        slab[None],
        kernel,
        (1, 1, 1),
        [(0, 0), (1, 1), (1, 1)],
        dimension_numbers=("NCDHW", "OIDHW", "NCDHW"),
        preferred_element_type=jnp.float32,
    )[0]


def plane_shifts(upstream):
    height = upstream.shape[2]
    length = upstream.shape[3]
    spread = jnp.pad(upstream, ((0, 0), (0, 0), (1, 1), (1, 1)))
    copies = []
    for tap in range(9):
        second = tap // 3
        third = tap % 3
        copies.append(
            spread[:, :, 2 - second : 2 - second + height, 2 - third : 2 - third + length]
        )
    stacked = jnp.stack(copies, 1)
    return stacked.reshape(upstream.shape[0] * 9, -1)


def tap_grads(rimmed, shifted, out_dev, depth):
    rows = []
    for first in range(3):
        window = lax.slice_in_dim(rimmed, first, first + depth, axis=1)
        flat = window.reshape(window.shape[0], -1)
        product = lax.dot_general(
            shifted, flat, (((1,), (1,)), ((), ())), preferred_element_type=jnp.float32
        )
        rows.append(product.reshape(out_dev, 9, window.shape[0]))
    return jnp.concatenate(rows, axis=1)


def line_steps(block, axis):
    count = lax.axis_size(axis)
    lefts, rights = [], []
    from_left = block
    from_right = block
    for step in range(1, count):
        from_left = lax.ppermute(
            from_left, axis, [(i, i + 1) for i in range(step - 1, count - 1)]
        )
        from_right = lax.ppermute(
            from_right, axis, [(i, i - 1) for i in range(1, count - step + 1)]
        )
        lefts.append(from_left)
        rights.append(from_right)
    return lefts, rights


def line_gather(block, axis, lefts, rights):
    count = lax.axis_size(axis)
    here = lax.axis_index(axis)
    blocks = [block]
    for k in range(1, count):
        blocks.append(jnp.where(here + k < count, rights[k - 1], lefts[count - k - 1]))
    return jnp.concatenate(blocks, axis=0)


def space_sum(grads, beside=None, operand=None, early=None):
    count = lax.axis_size("space")
    result = None
    if count != 4 or grads.shape[0] % 2:
        if beside is not None:
            result = beside(operand)
        return lax.psum(grads, "space"), result, early
    core = lax.axis_index("space") % 2
    half = grads.shape[0] // 2
    pair = [(i, i ^ 1) for i in range(count)]
    across = [(i, i ^ 2) for i in range(count)]
    mine = lax.dynamic_slice_in_dim(grads, core * half, half, axis=0)
    other = lax.dynamic_slice_in_dim(grads, (1 - core) * half, half, axis=0)
    mine = mine + lax.ppermute(other, "space", pair)
    if early is not None:
        mine, early = lax.optimization_barrier((mine, early))
    if beside is not None:
        mine, operand = lax.optimization_barrier((mine, operand))
    arrived = lax.ppermute(mine, "space", across)
    if beside is not None:
        result = beside(operand)
        arrived, result = lax.optimization_barrier((arrived, result))
    mine = mine + arrived
    theirs = lax.ppermute(mine, "space", pair)
    low = jnp.where(core == 0, mine, theirs)
    high = jnp.where(core == 0, theirs, mine)
    return jnp.concatenate([low, high], axis=0), result, early


def on_device(volume, weight, bias, upstream):
    out_dev = weight.shape[0]
    in_all = weight.shape[2]
    in_dev = volume.shape[0]
    depth = upstream.shape[1]
    kernel = weight.reshape(out_dev, 3, 3, 3, in_all).transpose(0, 4, 1, 2, 3)
    shifted = plane_shifts(upstream)
    lefts, rights = line_steps(volume, "filt")
    own = padded(volume, (("space", 1),), 1)
    first = min(2, len(lefts))
    tied = lax.optimization_barrier((own, lefts[:first], rights[:first]))
    own, lefts[:first], rights[:first] = tied
    own_grads, _, _ = space_sum(tap_grads(own, shifted, out_dev, depth))
    rolled = line_gather(volume, "filt", lefts, rights)
    rolled = padded(rolled, (("space", 1),), 1)
    start = lax.axis_index("filt") * in_dev
    rest = lax.slice_in_dim(rolled, in_dev, in_all, axis=0)

    def forward(slab):
        slab = jnp.roll(slab, start, axis=0)
        pre = convolve(slab, kernel) + bias[:, None, None, None]
        return jnp.where(pre > 0, pre, 0.3 * pre).astype(jnp.bfloat16)

    rest_grads, features, own_grads = space_sum(
        tap_grads(rest, shifted, out_dev, depth), forward, rolled, early=own_grads
    )
    ordered = jnp.concatenate([own_grads, rest_grads], axis=2)
    blocks = in_all // in_dev
    here = lax.axis_index("filt")
    pieces = [
        lax.dynamic_slice_in_dim(ordered, ((g - here) % blocks) * in_dev, in_dev, axis=2)
        for g in range(blocks)
    ]
    weight_grad = jnp.concatenate(pieces, axis=2)
    return (features, weight_grad)


def solution(mesh):
    return jax.shard_map(
        on_device,
        mesh=mesh,
        in_specs=(
            P("filt", ("parts", "space"), None, None),
            P("filt", None, None),
            P("filt"),
            P("filt", ("parts", "space"), None, None),
        ),
        out_specs=(P("filt", ("parts", "space"), None, None), P(("parts", "filt"), None, None)),
        check_vma=False,
    )
```

```python
import jax
import jax.numpy as jnp
from jax import lax
from jax.sharding import PartitionSpec as P


def padded(block, sides, width):
    for axis, dim in sides:
        count = lax.axis_size(axis)
        forward = [(i, i + 1) for i in range(count - 1)]
        backward = [(target, source) for source, target in forward]
        low = lax.ppermute(
            lax.slice_in_dim(block, block.shape[dim] - width, None, axis=dim), axis, forward
        )
        high = lax.ppermute(lax.slice_in_dim(block, 0, width, axis=dim), axis, backward)
        block = jnp.concatenate([low, block, high], axis=dim)
    return block


def convolve(slab, kernel):
    return lax.conv_general_dilated(
        slab[None],
        kernel,
        (1, 1, 1),
        [(0, 0), (1, 1), (1, 1)],
        dimension_numbers=("NCDHW", "OIDHW", "NCDHW"),
        preferred_element_type=jnp.float32,
    )[0]


def plane_shifts(upstream):
    height = upstream.shape[2]
    length = upstream.shape[3]
    spread = jnp.pad(upstream, ((0, 0), (0, 0), (1, 1), (1, 1)))
    copies = []
    for tap in range(9):
        second = tap // 3
        third = tap % 3
        copies.append(
            spread[:, :, 2 - second : 2 - second + height, 2 - third : 2 - third + length]
        )
    stacked = jnp.stack(copies, 1)
    return stacked.reshape(upstream.shape[0] * 9, -1)


def tap_grads(rimmed, shifted, out_dev, depth):
    rows = []
    for first in range(3):
        window = lax.slice_in_dim(rimmed, first, first + depth, axis=1)
        flat = window.reshape(window.shape[0], -1)
        product = lax.dot_general(
            shifted, flat, (((1,), (1,)), ((), ())), preferred_element_type=jnp.float32
        )
        rows.append(product.reshape(out_dev, 9, window.shape[0]))
    return jnp.concatenate(rows, axis=1)


def line_steps(block, axis):
    count = lax.axis_size(axis)
    lefts, rights = [], []
    from_left = block
    from_right = block
    for step in range(1, count):
        from_left = lax.ppermute(
            from_left, axis, [(i, i + 1) for i in range(step - 1, count - 1)]
        )
        from_right = lax.ppermute(
            from_right, axis, [(i, i - 1) for i in range(1, count - step + 1)]
        )
        lefts.append(from_left)
        rights.append(from_right)
    return lefts, rights


def line_gather(block, axis, lefts, rights):
    count = lax.axis_size(axis)
    here = lax.axis_index(axis)
    blocks = [block]
    for k in range(1, count):
        blocks.append(jnp.where(here + k < count, rights[k - 1], lefts[count - k - 1]))
    return jnp.concatenate(blocks, axis=0)


def space_sum(grads, beside=None, operand=None, early=None):
    count = lax.axis_size("space")
    result = None
    if count != 4 or grads.shape[0] % 2:
        if beside is not None:
            result = beside(operand)
        return lax.psum(grads, "space"), result, early
    core = lax.axis_index("space") % 2
    half = grads.shape[0] // 2
    pair = [(i, i ^ 1) for i in range(count)]
    across = [(i, i ^ 2) for i in range(count)]
    mine = lax.dynamic_slice_in_dim(grads, core * half, half, axis=0)
    other = lax.dynamic_slice_in_dim(grads, (1 - core) * half, half, axis=0)
    mine = mine + lax.ppermute(other, "space", pair)
    if early is not None:
        mine, early = lax.optimization_barrier((mine, early))
    arrived = lax.ppermute(mine, "space", across)
    if beside is not None:
        result = beside(operand)
        arrived, result = lax.optimization_barrier((arrived, result))
    mine = mine + arrived
    theirs = lax.ppermute(mine, "space", pair)
    low = jnp.where(core == 0, mine, theirs)
    high = jnp.where(core == 0, theirs, mine)
    return jnp.concatenate([low, high], axis=0), result, early


def on_device(volume, weight, bias, upstream):
    out_dev = weight.shape[0]
    in_all = weight.shape[2]
    in_dev = volume.shape[0]
    depth = upstream.shape[1]
    kernel = weight.reshape(out_dev, 3, 3, 3, in_all).transpose(0, 4, 1, 2, 3)
    shifted = plane_shifts(upstream)
    lefts, rights = line_steps(volume, "filt")
    own = padded(volume, (("space", 1),), 1)
    first = min(2, len(lefts))
    tied = lax.optimization_barrier((own, lefts[:first], rights[:first]))
    own, lefts[:first], rights[:first] = tied
    own_grads, _, _ = space_sum(tap_grads(own, shifted, out_dev, depth))
    rolled = line_gather(volume, "filt", lefts, rights)
    rolled = padded(rolled, (("space", 1),), 1)
    start = lax.axis_index("filt") * in_dev
    rimmed = jnp.roll(rolled, start, axis=0)
    rest = lax.slice_in_dim(rolled, in_dev, in_all, axis=0)

    def forward(slab):
        pre = convolve(slab, kernel) + bias[:, None, None, None]
        return jnp.where(pre > 0, pre, 0.3 * pre).astype(jnp.bfloat16)

    rest_grads, features, own_grads = space_sum(
        tap_grads(rest, shifted, out_dev, depth), forward, rimmed, early=own_grads
    )
    ordered = jnp.concatenate([own_grads, rest_grads], axis=2)
    blocks = in_all // in_dev
    here = lax.axis_index("filt")
    pieces = [
        lax.dynamic_slice_in_dim(ordered, ((g - here) % blocks) * in_dev, in_dev, axis=2)
        for g in range(blocks)
    ]
    weight_grad = jnp.concatenate(pieces, axis=2)
    return (features, weight_grad)


def solution(mesh):
    return jax.shard_map(
        on_device,
        mesh=mesh,
        in_specs=(
            P("filt", ("parts", "space"), None, None),
            P("filt", None, None),
            P("filt"),
            P("filt", ("parts", "space"), None, None),
        ),
        out_specs=(P("filt", ("parts", "space"), None, None), P(("parts", "filt"), None, None)),
        check_vma=False,
    )
```
